512 devices in a mesh: gx: 32 (over z, core), gy: 4 (over y), gz: 4 (over x).
Axes of the slice: x: 4, y: 4, z: 16, core: 2. Of those that a mesh axis runs over, the one named last changes fastest.
Arguments:
- saturation: float32 [64, 512, 512], P('gz', 'gx', 'gy'), may hold values from 0.05 to 0.95
- retention: float32 [64, 512, 512], P('gz', 'gx', 'gy'), may hold values from 0 to 1
- gravity: float32 [64, 512, 512], P('gz', 'gx', 'gy'), may hold values from 0.02 to 0.2
- cell_map: int32 [4, 32768, 128], P('gz', ('gx', 'gy')), may hold values from 0 to 1023
- owner_id: int32 [4, 16384, 1], P('gz', ('gx', 'gy')), may hold values from 0 to 127; in each aligned block of 128 rows (0 to 127, 128 to 255, ..., all dimensions but the last counted through in order) at most 2 rows name the same one
- stream_dir: int32 [4, 8192], P('gz', ('gx', 'gy')), may hold values 0 or 1
- node_weight: float32 [4, 16384, 128], P('gz', ('gx', 'gy')), may hold values from 0.25 to 4
- flight: float32 [4, 16384, 128], P('gz', ('gx', 'gy')), may hold values from 0.1 to 0.45
Outputs:
- final_sat: float32 [64, 512, 512], P('gz', 'gx', 'gy')
- streamline_sat: float32 [4, 16384, 128], P('gz', ('gx', 'gy'))
The draws below stay inside these ranges and needn't reach their ends.
Inputs may be any that keep to these rules, and one draw needn't show every extreme that they name: `owner_id`: among the 128 segments of one device no owner is named more than 2 times; some owner exactly 2 times.
All inputs are finite; a program needn't handle non-finite values. No bound on the sum of `stream_dir` on one device may be relied on, other than what follows from the above.
Results may differ from the reference program's by a relative error of at most 0.00005.
Values sent between devices are 32-bit elements; how exact they have to be, the bound alone decides.
No kernel may reach another device: no remote copies, remote signals or barrier semaphores. Data moves between devices by JAX's collectives and lax.ppermute only.
A program may use at most 64 MiB of HBM per device.

```python
import math
import jax
import jax.numpy as jnp
import numpy as np
from jax import lax

CZ = 16
CX = 16
CY = 128
SEG_DEV = 128
SEG_LEN = 128
BL_STEPS = 8
GROUPS = 128
CAP = 2
STREAMS_DEV = 64
MAP_CELLS = 1024
DEPTH_LAYERS = 64
CELLS_ALONG_X = 512
CELLS_ALONG_Y = 512
N_GX = 32
N_GY = 4
N_GZ = 4


def draw_retention(key, part):
    sorting_keys = jax.random.split(key, 6)
    picker = jax.random.uniform(sorting_keys[0], (CELLS_ALONG_X, CELLS_ALONG_Y))
    slow = picker < 0.5
    slow_rate = jnp.log(10.0) * jax.random.uniform(sorting_keys[1], (CELLS_ALONG_X, CELLS_ALONG_Y), minval=0.2, maxval=0.8) / DEPTH_LAYERS
    fast_rate = 3.0 / jax.random.uniform(sorting_keys[2], (CELLS_ALONG_X, CELLS_ALONG_Y), minval=30.0, maxval=50.0)
    base = jnp.where(slow, slow_rate, fast_rate)
    rough = jax.random.uniform(sorting_keys[3], (DEPTH_LAYERS, CELLS_ALONG_X, CELLS_ALONG_Y), minval=0.5, maxval=1.5)
    retained_rows = jnp.exp(-base[None] * rough)
    segment_bundle = jax.random.uniform(sorting_keys[4], (DEPTH_LAYERS, CELLS_ALONG_X, CELLS_ALONG_Y)) < 3.0 / DEPTH_LAYERS
    segment_divider = jax.random.uniform(sorting_keys[5], (DEPTH_LAYERS, CELLS_ALONG_X, CELLS_ALONG_Y), minval=0.5, maxval=0.8)
    return jnp.where(segment_bundle, retained_rows * segment_divider, retained_rows).astype(jnp.float32)


def with_ends(values, rng, least, largest):
    longest = values.shape.index(max(values.shape))
    spots = []
    for shift in (0, 1):
        where = [jax.random.randint(jax.random.fold_in(rng, axis), (), 0, length) for axis, length in enumerate(values.shape)]
        where[longest] = (where[longest] + shift) % values.shape[longest]
        spots.append(tuple(where))
    return values.at[spots[0]].set(least).at[spots[1]].set(largest)


def levels(stream_key, shape, pieces, low, high):
    def one(position, shards_of):
        draws = jax.random.uniform(jax.random.fold_in(jax.random.fold_in(stream_key, 6), position), (shards_of,), jnp.float32, low / len(pieces), high / len(pieces))
        return jnp.repeat(jnp.exp(draws), shape[position] // shards_of).reshape((-1,) + (1,) * (len(shape) - position - 1))

    gain = one(*pieces[0])
    for cut in pieces[1:]:
        gain = gain * one(*cut)
    return gain


def routed_block(key, own, number, rows, count, top, most, slope):
    ranking = jax.random.permutation(key, count)
    packed, ordinary = shares(count, rows * top, most, slope, True), shares(count, rows * top, most, slope, False)
    places = jnp.arange(count)

    def named(tallies, turn):
        used = int((tallies > 0).sum())
        fixed = max(1, used // 4)
        shifted = fixed + (places - fixed + turn * (used - fixed)) % max(1, count - fixed)
        return jnp.zeros((count,), jnp.int32).at[ranking[jnp.where(places < fixed, places, shifted)]].set(jnp.asarray(tallies, jnp.int32))

    tallies = jnp.where(number % 4 == 0, named(packed, number // 4), named(ordinary, number - number // 4 - 1))
    mixed = jax.random.permutation(jax.random.fold_in(own, 3), count)
    donor, taker = mixed[0:count // 2 * 2:2], mixed[1:count // 2 * 2:2]
    margin = jnp.minimum(tallies[donor] - 1, most - tallies[taker]) // 2
    margin = jnp.where((donor == ranking[0]) | (taker == ranking[0]) | (tallies[taker] == 0), 0, jnp.maximum(margin, 0))
    shifted = jax.random.randint(jax.random.fold_in(own, 4), (count // 2,), 0, 1 << 20) % (margin + 1)
    tallies = tallies.at[donor].add(-shifted).at[taker].add(shifted)
    labels = jnp.searchsorted(jnp.cumsum(tallies), jnp.arange(rows * top), side="right").astype(jnp.int32)
    table = labels.reshape(top, rows).T
    table = table[jax.random.permutation(jax.random.fold_in(own, 1), rows)]
    turn = jax.random.randint(jax.random.fold_in(own, 2), (rows, 1), 0, top)
    return jnp.take_along_axis(table, (jnp.arange(top)[None, :] + turn) % top, axis=1)


def shares(count, total, bound, skew, full):
    portions = [(1 << 20) // math.isqrt(standing ** skew) + 1 for standing in range(1, count + 1)]
    largest = bound if full else min(bound, max(-(-total // count), total * portions[0] // sum(portions)))
    least = 1 if total - largest >= count - 1 else 0
    counts, spare = [largest] + [least] * (count - 1), total - largest - least * (count - 1)
    while spare > 0:
        movable = [i for i in range(1, count) if counts[i] < largest] or [i for i in range(1, count) if counts[i] < bound]
        whole, remaining = sum([portions[i] for i in movable]), spare
        for i in movable:
            more = min(bound - counts[i], max(1, remaining * portions[i] // whole), spare)
            counts[i] = counts[i] + more
            spare = spare - more
    return np.array(counts)


def setup_inputs(seed: int = 0) -> dict:
    key_list = jax.random.split(jax.random.key(seed), 9)
    saturation = jnp.clip(0.05 + 0.9 * jax.random.uniform(key_list[0], (DEPTH_LAYERS, CELLS_ALONG_X, CELLS_ALONG_Y), jnp.float32) ** levels(key_list[0], (DEPTH_LAYERS, CELLS_ALONG_X, CELLS_ALONG_Y), ((0, 4), (1, 32), (2, 4)), -0.2, 0.2), 0.05, 0.95)
    retention = draw_retention(jax.random.fold_in(key_list[8], 71), 0)
    gravity = jnp.clip(jnp.exp(math.log(0.2) - 2.3025851 * jax.random.uniform(key_list[2], (DEPTH_LAYERS, CELLS_ALONG_X, CELLS_ALONG_Y), jnp.float32) ** levels(key_list[2], (DEPTH_LAYERS, CELLS_ALONG_X, CELLS_ALONG_Y), ((0, 4), (1, 32), (2, 4)), -0.2, 0.2)), 0.02, 0.2)
    cell_map = with_ends(jax.random.randint(key_list[3], (N_GZ, GROUPS * GROUPS * CAP, SEG_LEN), 0, MAP_CELLS), jax.random.fold_in(key_list[3], 1), 0, MAP_CELLS - 1).astype(jnp.int32)
    owner_id_keys = jax.random.split(jax.random.fold_in(key_list[4], 1), N_GZ * (GROUPS * SEG_DEV) // SEG_DEV)
    owner_id_turns = jax.random.permutation(jax.random.fold_in(key_list[4], 3), N_GZ * (GROUPS * SEG_DEV) // SEG_DEV)
    owner_id = jax.vmap(lambda own, number: routed_block(jax.random.fold_in(key_list[4], 2), own, number, SEG_DEV, GROUPS, 1, CAP, 2))(owner_id_keys, owner_id_turns).reshape((N_GZ, GROUPS * SEG_DEV, 1))
    stream_dir = with_ends((jax.random.randint(key_list[5], (N_GZ, GROUPS * STREAMS_DEV), 0, 2) < 1).astype(jnp.int32), jax.random.fold_in(key_list[5], 1), 0, 1)
    node_weight = jnp.clip(jnp.exp(math.log(4.0) - 2.7725887 * jax.random.uniform(key_list[6], (N_GZ, GROUPS * SEG_DEV, SEG_LEN), jnp.float32) ** levels(key_list[6], (N_GZ, GROUPS * SEG_DEV, SEG_LEN), ((0, 4), (1, 128)), -0.2, 0.2)), 0.25, 4.0)
    flight = jnp.clip(0.1 + 0.35 * jax.random.uniform(key_list[7], (N_GZ, GROUPS * SEG_DEV, SEG_LEN), jnp.float32) ** levels(key_list[7], (N_GZ, GROUPS * SEG_DEV, SEG_LEN), ((0, 4), (1, 128)), -0.2, 0.2), 0.1, 0.45)
    return {"saturation": saturation, "retention": retention, "gravity": gravity, "cell_map": cell_map, "owner_id": owner_id, "stream_dir": stream_dir, "node_weight": node_weight, "flight": flight}


def frac_flow(values):
    return values * values / (values * values + (1.0 - values) * (1.0 - values))


def transport(node_sat, increments, reversed_flag):
    flipped = reversed_flag[..., None] == 1
    state = jnp.where(flipped, node_sat[..., ::-1], node_sat)
    ratio = jnp.where(flipped, increments[..., ::-1], increments)
    inlet = jnp.ones(state.shape[:-1] + (1,), jnp.float32)
    for iteration in range(BL_STEPS):
        flows = frac_flow(state)
        upstream = jnp.concatenate([inlet, flows[..., :-1]], axis=-1)
        state = state - ratio * (flows - upstream)
    return jnp.where(flipped, state[..., ::-1], state)


def reference(saturation, retention, gravity, cell_map, owner_id, stream_dir, node_weight, flight):
    groups = N_GX * N_GY
    blocks = saturation.reshape(N_GZ, CZ, N_GX, CX, N_GY, CY).transpose(0, 2, 4, 1, 3, 5).reshape(N_GZ, groups, CZ * CX * CY)
    owners = owner_id[..., 0].reshape(N_GZ, groups, SEG_DEV)
    onehot = (owners[..., None] == jnp.arange(groups, dtype=jnp.int32)).astype(jnp.int32)
    before = jnp.cumsum(onehot, axis=-2) - onehot
    slot = jnp.sum(before * onehot, axis=-1)
    source = jnp.arange(groups, dtype=jnp.int32)[None, :, None]
    slab = jnp.arange(N_GZ, dtype=jnp.int32)[:, None, None]
    table = cell_map.reshape(N_GZ, groups, groups * CAP, SEG_LEN)
    cell_ids = table[slab, owners, source * CAP + slot]
    node_in = blocks[slab[..., None], owners[..., None], cell_ids]
    lines = node_in.reshape(N_GZ, groups, STREAMS_DEV, 2 * SEG_LEN)
    ratio = flight.reshape(N_GZ, groups, STREAMS_DEV, 2 * SEG_LEN)
    flags = stream_dir.reshape(N_GZ, groups, STREAMS_DEV)
    updated = transport(lines, ratio, flags).reshape(N_GZ, groups, SEG_DEV, SEG_LEN)
    weights = node_weight.reshape(N_GZ, groups, SEG_DEV, SEG_LEN)
    empty = jnp.zeros((N_GZ, groups, CZ * CX * CY), jnp.float32)
    numerator = empty.at[slab[..., None], owners[..., None], cell_ids].add(weights * updated)
    denominator = empty.at[slab[..., None], owners[..., None], cell_ids].add(weights)
    mixed_blocks = (blocks + numerator) / (1.0 + denominator)
    mixed = mixed_blocks.reshape(N_GZ, N_GX, N_GY, CZ, CX, CY).transpose(0, 3, 1, 4, 2, 5).reshape(DEPTH_LAYERS, CELLS_ALONG_X, CELLS_ALONG_Y)
    burden = gravity * saturation * (1.0 - saturation)

    def descend(carried, layer):
        keep, drop = layer
        inflow = keep * carried
        return inflow + drop, inflow

    _, inflow = lax.scan(descend, jnp.zeros((CELLS_ALONG_X, CELLS_ALONG_Y), jnp.float32), (retention, burden))
    final_sat = mixed + inflow - burden
    return final_sat, updated.reshape(N_GZ, groups * SEG_DEV, SEG_LEN)
```

```python
import math

import jax
import jax.numpy as jnp
from jax import lax
from jax.experimental import pallas as pl
from jax.experimental.pallas import tpu as pltpu
from jax.sharding import PartitionSpec as P

BL_STEPS = 8


def from_behind(block, axis, distance):
    devices = range(lax.axis_size(axis))
    route = [(i - distance, i) for i in devices if i - distance in devices]
    return lax.ppermute(block, axis, route)


def frac_flow(values):
    return values * values / (values * values + (1.0 - values) * (1.0 - values))


def transport(node_sat, increments, reversed_flag):
    flipped = reversed_flag[..., None] == 1
    state = jnp.where(flipped, node_sat[..., ::-1], node_sat)
    ratio = jnp.where(flipped, increments[..., ::-1], increments)
    inlet = jnp.ones(state.shape[:-1] + (1,), jnp.float32)
    for iteration in range(BL_STEPS):
        flows = frac_flow(state)
        upstream = jnp.concatenate([inlet, flows[..., :-1]], axis=-1)
        state = state - ratio * (flows - upstream)
    return jnp.where(flipped, state[..., ::-1], state)


def slot_rows(owners, groups, capacity):
    onehot = (owners[:, None] == jnp.arange(groups, dtype=jnp.int32)[None, :]).astype(jnp.int32)
    before = jnp.cumsum(onehot, axis=0) - onehot
    return owners * capacity + jnp.sum(before * onehot, axis=1)


def descend(carried, layer):
    keep, drop = layer
    inflow = keep * carried
    return (inflow + drop, inflow)


def column_hot(cell_ids):
    lanes = lax.broadcasted_iota(jnp.int32, (128, cell_ids.shape[0]), 0)
    return (cell_ids[None, :] % 128 == lanes).astype(jnp.float32)


def row_hot(cell_ids, map_rows):
    levels = lax.broadcasted_iota(jnp.int32, (map_rows, cell_ids.shape[0]), 0)
    return (cell_ids[None, :] // 128 == levels).astype(jnp.float32)


def gather_kernel(table_ref, ids_ref, out_ref):
    map_rows = table_ref.shape[0]
    tiles = ids_ref.shape[0] // 8
    table = table_ref[...]
    spread = [jnp.broadcast_to(table[r : r + 1, :], (8, 128)) for r in range(map_rows)]

    def body(i, carry):
        start = pl.multiple_of(i * 8, 8)
        ids = ids_ref[pl.ds(start, 8), :]
        lane = jnp.bitwise_and(ids, 127)
        level = jnp.right_shift(ids, 7)
        picked = jnp.zeros((8, 128), jnp.float32)
        for r in range(map_rows):
            got = jnp.take_along_axis(spread[r], lane, axis=1, mode="promise_in_bounds")
            picked = jnp.where(level == r, got, picked)
        out_ref[pl.ds(start, 8), :] = picked
        return carry

    lax.fori_loop(0, tiles, body, 0, unroll=4)


def gather_cells(cell_table, local_map):
    return pl.pallas_call(
        gather_kernel,
        out_shape=jax.ShapeDtypeStruct(local_map.shape, jnp.float32),
        in_specs=[pl.BlockSpec(memory_space=pltpu.VMEM)] * 2,
        out_specs=pl.BlockSpec(memory_space=pltpu.VMEM),
    )(cell_table, local_map)


def scatter_kernel(ids_ref, upper_ref, lower_ref, out_ref):
    map_rows = out_ref.shape[0] // 2
    tiles = ids_ref.shape[0] // 8
    lanes = lax.broadcasted_iota(jnp.int32, (128, 128), 0)
    levels = lax.broadcasted_iota(jnp.int32, (map_rows, 128), 0)

    def pieces(values):
        high = values.astype(jnp.bfloat16)
        rest = values - high.astype(jnp.float32)
        middle = rest.astype(jnp.bfloat16)
        low = (rest - middle.astype(jnp.float32)).astype(jnp.bfloat16)
        return [high, middle, low]

    def body(i, totals):
        start = pl.multiple_of(i * 8, 8)
        ids = ids_ref[pl.ds(start, 8), :]
        upper = upper_ref[pl.ds(start, 8), :]
        lower = lower_ref[pl.ds(start, 8), :]
        hots, parts = [], []
        for j in range(8):
            cell = ids[j : j + 1, :]
            hots.append((jnp.bitwise_and(cell, 127) == lanes).astype(jnp.bfloat16))
            on_level = jnp.right_shift(cell, 7) == levels
            rows = jnp.concatenate(
                [
                    jnp.where(on_level, upper[j : j + 1, :], 0.0),
                    jnp.where(on_level, lower[j : j + 1, :], 0.0),
                ],
                axis=0,
            )
            parts.append(jnp.concatenate(pieces(rows), axis=0))
        added = lax.dot_general(
            jnp.concatenate(parts, axis=1),
            jnp.concatenate(hots, axis=1),
            (((1,), (1,)), ((), ())),
            preferred_element_type=jnp.float32,
        )
        return totals + added

    totals = lax.fori_loop(
        0, tiles, body, jnp.zeros((6 * map_rows, 128), jnp.float32), unroll=2
    )
    span = 2 * map_rows
    out_ref[...] = (totals[:span] + totals[span : 2 * span]) + totals[2 * span :]


def scatter_cells(local_map, upper, lower, map_rows):
    return pl.pallas_call(
        scatter_kernel,
        out_shape=jax.ShapeDtypeStruct((2 * map_rows, 128), jnp.float32),
        in_specs=[pl.BlockSpec(memory_space=pltpu.VMEM)] * 3,
        out_specs=pl.BlockSpec(memory_space=pltpu.VMEM),
    )(local_map, upper, lower)


def on_device(saturation, retention, gravity, cell_map, owner_id, stream_dir, node_weight, flight):
    layers, rows_x, rows_y = saturation.shape
    size_x = lax.axis_size("gx")
    size_y = lax.axis_size("gy")
    groups = size_x * size_y
    seg_len = cell_map.shape[2]
    capacity = cell_map.shape[1] // groups
    flat = saturation.reshape(-1)
    cell_count = flat.shape[0]
    map_rows = min(cell_count // 128, max(8, capacity * seg_len // 32))
    local_map = cell_map[0]
    node_total = local_map.shape[0] * seg_len
    block_width = math.gcd(node_total, 2048)
    block_count = node_total // block_width
    block_ids = local_map.reshape(block_count, block_width)
    cell_table = flat[: map_rows * 128].reshape(map_rows, 128)

    offered = gather_cells(cell_table, local_map)
    arrived = lax.all_to_all(offered, ("gx", "gy"), split_axis=0, concat_axis=0, tiled=True)
    burden = gravity * saturation * (1.0 - saturation)
    zero_plane = jnp.zeros((rows_x, rows_y), jnp.float32)
    local_end, _ = lax.scan(descend, zero_plane, (retention, burden))
    through = jnp.prod(retention, axis=0)

    depth_size = lax.axis_size("gz")
    pair = jnp.stack([through, local_end])
    behind = [from_behind(pair, "gz", d) for d in range(1, depth_size)]
    entering = zero_plane
    for d in range(depth_size - 1, 0, -1):
        above = behind[d - 1]
        entering = above[0] * entering + above[1]
    _, inflow = lax.scan(descend, entering, (retention, burden))
    owners = owner_id[0, :, 0]
    rows = slot_rows(owners, groups, capacity)
    node_in = arrived[rows]
    seg_dev = node_in.shape[0]
    updated = transport(
        node_in.reshape(seg_dev // 2, 2 * seg_len),
        flight[0].reshape(seg_dev // 2, 2 * seg_len),
        stream_dir[0],
    )
    updated = updated.reshape(seg_dev, seg_len)
    weights = node_weight[0]
    slots = groups * capacity
    filled = rows[None, :] == jnp.arange(slots, dtype=jnp.int32)[:, None]
    source = jnp.sum(jnp.where(filled, jnp.arange(seg_dev, dtype=jnp.int32)[None, :], 0), axis=1)
    used = jnp.any(filled, axis=1)
    stacked = jnp.stack([weights * updated, weights], axis=1)
    package = jnp.where(used[:, None, None], stacked[source], 0.0)
    returned = lax.all_to_all(package, ("gx", "gy"), split_axis=0, concat_axis=0, tiled=True)
    sums = scatter_cells(local_map, returned[:, 0, :], returned[:, 1, :], map_rows)
    padding = jnp.zeros((cell_count - map_rows * 128,), jnp.float32)
    numerator = jnp.concatenate([sums[:map_rows].reshape(-1), padding])
    denominator = jnp.concatenate([sums[map_rows:].reshape(-1), padding])
    mixed = ((flat + numerator) / (1.0 + denominator)).reshape(layers, rows_x, rows_y)
    final_sat = mixed + inflow - burden
    return (final_sat, updated[None])


def solution(mesh):
    return jax.shard_map(
        on_device,
        mesh=mesh,
        in_specs=(
            P("gz", "gx", "gy"),
            P("gz", "gx", "gy"),
            P("gz", "gx", "gy"),
            P("gz", ("gx", "gy"), None),
            P("gz", ("gx", "gy"), None),
            P("gz", ("gx", "gy")),
            P("gz", ("gx", "gy"), None),
            P("gz", ("gx", "gy"), None),
        ),
        out_specs=(P("gz", "gx", "gy"), P("gz", ("gx", "gy"), None)),
        check_vma=False,
    )
```

```python
import jax
import jax.numpy as jnp
from jax import lax
from jax.experimental import pallas as pl
from jax.experimental.pallas import tpu as pltpu
from jax.sharding import PartitionSpec as P


BL_STEPS = 8


def from_behind(block, axis, distance):
    devices = range(lax.axis_size(axis))
    route = [(i - distance, i) for i in devices if i - distance in devices]
    return lax.ppermute(block, axis, route)


def frac_flow(values):
    return values * values / (values * values + (1.0 - values) * (1.0 - values))


def transport(node_sat, increments, reversed_flag):
    flipped = reversed_flag[..., None] == 1
    state = jnp.where(flipped, node_sat[..., ::-1], node_sat)
    ratio = jnp.where(flipped, increments[..., ::-1], increments)
    inlet = jnp.ones(state.shape[:-1] + (1,), jnp.float32)
    for _ in range(BL_STEPS):
        flows = frac_flow(state)
        upstream = jnp.concatenate([inlet, flows[..., :-1]], axis=-1)
        state = state - ratio * (flows - upstream)
    return jnp.where(flipped, state[..., ::-1], state)


def slot_rows(owners, groups, capacity):
    onehot = (owners[:, None] == jnp.arange(groups, dtype=jnp.int32)[None, :]).astype(jnp.int32)
    before = jnp.cumsum(onehot, axis=0) - onehot
    return owners * capacity + jnp.sum(before * onehot, axis=1)


def descend(carried, layer):
    keep, drop = layer
    inflow = keep * carried
    return (inflow + drop, inflow)


def gather_kernel(table_ref, ids_ref, out_ref):
    map_rows = table_ref.shape[0]
    tiles = ids_ref.shape[0] // 8
    table = table_ref[...]
    spread = [jnp.broadcast_to(table[r : r + 1, :], (8, 128)) for r in range(map_rows)]

    def body(i, carry):
        start = pl.multiple_of(i * 8, 8)
        ids = ids_ref[pl.ds(start, 8), :]
        lane = jnp.bitwise_and(ids, 127)
        level = jnp.right_shift(ids, 7)
        picked = jnp.zeros((8, 128), jnp.float32)
        for r in range(map_rows):
            got = jnp.take_along_axis(spread[r], lane, axis=1, mode="promise_in_bounds")
            picked = jnp.where(level == r, got, picked)
        out_ref[pl.ds(start, 8), :] = picked
        return carry

    lax.fori_loop(0, tiles, body, 0, unroll=4)


def gather_cells(cell_table, local_map):
    return pl.pallas_call(
        gather_kernel,
        out_shape=jax.ShapeDtypeStruct(local_map.shape, jnp.float32),
        in_specs=[pl.BlockSpec(memory_space=pltpu.VMEM)] * 2,
        out_specs=pl.BlockSpec(memory_space=pltpu.VMEM),
    )(cell_table, local_map)


def scatter_kernel(ids_ref, upper_ref, lower_ref, out_ref):
    map_rows = out_ref.shape[0] // 2
    tiles = ids_ref.shape[0] // 8
    lanes = lax.broadcasted_iota(jnp.int32, (128, 128), 0)
    levels = lax.broadcasted_iota(jnp.int32, (map_rows, 128), 0)

    def pieces(values):
        high = values.astype(jnp.bfloat16)
        rest = values - high.astype(jnp.float32)
        middle = rest.astype(jnp.bfloat16)
        low = (rest - middle.astype(jnp.float32)).astype(jnp.bfloat16)
        return [high, middle, low]

    def body(i, totals):
        start = pl.multiple_of(i * 8, 8)
        ids = ids_ref[pl.ds(start, 8), :]
        upper = upper_ref[pl.ds(start, 8), :]
        lower = lower_ref[pl.ds(start, 8), :]
        hots, parts = [], []
        for j in range(8):
            cell = ids[j : j + 1, :]
            hots.append((jnp.bitwise_and(cell, 127) == lanes).astype(jnp.bfloat16))
            on_level = jnp.right_shift(cell, 7) == levels
            rows = jnp.concatenate(
                [
                    jnp.where(on_level, upper[j : j + 1, :], 0.0),
                    jnp.where(on_level, lower[j : j + 1, :], 0.0),
                ],
                axis=0,
            )
            parts.append(jnp.concatenate(pieces(rows), axis=0))
        added = lax.dot_general(
            jnp.concatenate(parts, axis=1),
            jnp.concatenate(hots, axis=1),
            (((1,), (1,)), ((), ())),
            preferred_element_type=jnp.float32,
        )
        return totals + added

    totals = lax.fori_loop(
        0, tiles, body, jnp.zeros((6 * map_rows, 128), jnp.float32), unroll=2
    )
    span = 2 * map_rows
    out_ref[...] = (totals[:span] + totals[span : 2 * span]) + totals[2 * span :]


def scatter_cells(local_map, upper, lower, map_rows):
    return pl.pallas_call(
        scatter_kernel,
        out_shape=jax.ShapeDtypeStruct((2 * map_rows, 128), jnp.float32),
        in_specs=[pl.BlockSpec(memory_space=pltpu.VMEM)] * 3,
        out_specs=pl.BlockSpec(memory_space=pltpu.VMEM),
    )(local_map, upper, lower)


def segregation(saturation, retention, gravity):
    burden = gravity * saturation * (1.0 - saturation)
    zero_plane = jnp.zeros(saturation.shape[1:], jnp.float32)
    local_end, _ = lax.scan(descend, zero_plane, (retention, burden))
    through = jnp.prod(retention, axis=0)
    depth_size = lax.axis_size("gz")
    pair = jnp.stack([through, local_end])
    behind = [from_behind(pair, "gz", d) for d in range(1, depth_size)]
    entering = zero_plane
    for d in range(depth_size - 1, 0, -1):
        above = behind[d - 1]
        entering = above[0] * entering + above[1]
    _, inflow = lax.scan(descend, entering, (retention, burden))
    return inflow, burden


def on_device(saturation, retention, gravity, cell_map, owner_id, stream_dir, node_weight, flight):
    layers, rows_x, rows_y = saturation.shape
    size_x = lax.axis_size("gx")
    size_y = lax.axis_size("gy")
    groups = size_x * size_y
    seg_len = cell_map.shape[2]
    capacity = cell_map.shape[1] // groups
    flat = saturation.reshape(-1)
    cell_count = flat.shape[0]
    map_rows = min(cell_count // 128, max(8, capacity * seg_len // 32))
    local_map = cell_map[0]
    cell_table = flat[: map_rows * 128].reshape(map_rows, 128)

    offered = gather_cells(cell_table, local_map)
    arrived = lax.all_to_all(offered, ("gx", "gy"), split_axis=0, concat_axis=0, tiled=True)
    owners = owner_id[0, :, 0]
    rows = slot_rows(owners, groups, capacity)
    node_in = arrived[rows]
    seg_dev = node_in.shape[0]
    updated = transport(
        node_in.reshape(seg_dev // 2, 2 * seg_len),
        flight[0].reshape(seg_dev // 2, 2 * seg_len),
        stream_dir[0],
    )
    updated = updated.reshape(seg_dev, seg_len)
    weights = node_weight[0]
    slots = groups * capacity
    filled = rows[None, :] == jnp.arange(slots, dtype=jnp.int32)[:, None]
    source = jnp.sum(jnp.where(filled, jnp.arange(seg_dev, dtype=jnp.int32)[None, :], 0), axis=1)
    used = jnp.any(filled, axis=1)
    stacked = jnp.stack([weights * updated, weights], axis=1)
    package = jnp.where(used[:, None, None], stacked[source], 0.0)
    returned = lax.all_to_all(package, ("gx", "gy"), split_axis=0, concat_axis=0, tiled=True)
    package, retention, gravity = lax.optimization_barrier((package, retention, gravity))
    inflow, burden = segregation(saturation, retention, gravity)
    sums = scatter_cells(local_map, returned[:, 0, :], returned[:, 1, :], map_rows)
    padding = jnp.zeros((cell_count - map_rows * 128,), jnp.float32)
    numerator = jnp.concatenate([sums[:map_rows].reshape(-1), padding])
    denominator = jnp.concatenate([sums[map_rows:].reshape(-1), padding])
    mixed = ((flat + numerator) / (1.0 + denominator)).reshape(layers, rows_x, rows_y)
    final_sat = mixed + inflow - burden
    return (final_sat, updated[None])


def solution(mesh):
    return jax.shard_map(
        on_device,
        mesh=mesh,
        in_specs=(
            P("gz", "gx", "gy"),
            P("gz", "gx", "gy"),
            P("gz", "gx", "gy"),
            P("gz", ("gx", "gy"), None),
            P("gz", ("gx", "gy"), None),
            P("gz", ("gx", "gy")),
            P("gz", ("gx", "gy"), None),
            P("gz", ("gx", "gy"), None),
        ),
        out_specs=(P("gz", "gx", "gy"), P("gz", ("gx", "gy"), None)),
        check_vma=False,
    )
```

```python
import jax
import jax.numpy as jnp
from jax import lax
from jax.experimental import pallas as pl
from jax.experimental.pallas import tpu as pltpu
from jax.sharding import PartitionSpec as P


BL_STEPS = 8


def from_behind(block, axis, distance):
    devices = range(lax.axis_size(axis))
    route = [(i - distance, i) for i in devices if i - distance in devices]
    return lax.ppermute(block, axis, route)


def frac_flow(values):
    return values * values / (values * values + (1.0 - values) * (1.0 - values))


def transport(node_sat, increments, reversed_flag):
    flipped = reversed_flag[..., None] == 1
    state = jnp.where(flipped, node_sat[..., ::-1], node_sat)
    ratio = jnp.where(flipped, increments[..., ::-1], increments)
    inlet = jnp.ones(state.shape[:-1] + (1,), jnp.float32)
    for _ in range(BL_STEPS):
        flows = frac_flow(state)
        upstream = jnp.concatenate([inlet, flows[..., :-1]], axis=-1)
        state = state - ratio * (flows - upstream)
    return jnp.where(flipped, state[..., ::-1], state)


def slot_rows(owners, groups, capacity):
    onehot = (owners[:, None] == jnp.arange(groups, dtype=jnp.int32)[None, :]).astype(jnp.int32)
    before = jnp.cumsum(onehot, axis=0) - onehot
    return owners * capacity + jnp.sum(before * onehot, axis=1)


def descend(carried, layer):
    keep, drop = layer
    inflow = keep * carried
    return (inflow + drop, inflow)


def gather_kernel(table_ref, ids_ref, out_ref):
    map_rows = table_ref.shape[1]
    tiles = ids_ref.shape[0] // 8
    table = table_ref[0]
    spread = [jnp.broadcast_to(table[r : r + 1, :], (8, 128)) for r in range(map_rows)]

    def body(i, carry):
        start = pl.multiple_of(i * 8, 8)
        ids = ids_ref[pl.ds(start, 8), :]
        lane = jnp.bitwise_and(ids, 127)
        level = jnp.right_shift(ids, 7)
        picked = jnp.zeros((8, 128), jnp.float32)
        for r in range(map_rows):
            got = jnp.take_along_axis(spread[r], lane, axis=1, mode="promise_in_bounds")
            picked = jnp.where(level == r, got, picked)
        out_ref[pl.ds(start, 8), :] = picked
        return carry

    lax.fori_loop(0, tiles, body, 0, unroll=True)


def gather_cells(saturation, local_map, map_rows):
    return pl.pallas_call(
        gather_kernel,
        out_shape=jax.ShapeDtypeStruct(local_map.shape, jnp.float32),
        grid=(1,),
        in_specs=[
            pl.BlockSpec((1, map_rows, 128), lambda i: (0, 0, 0)),
            pl.BlockSpec(local_map.shape, lambda i: (0, 0)),
        ],
        out_specs=pl.BlockSpec(local_map.shape, lambda i: (0, 0)),
    )(saturation, local_map)


def scatter_kernel(ids_ref, both_ref, out_ref):
    map_rows = out_ref.shape[0] // 2
    tiles = ids_ref.shape[0] // 8
    lanes = lax.broadcasted_iota(jnp.int32, (128, 128), 0)
    levels = lax.broadcasted_iota(jnp.int32, (map_rows, 128), 0)

    def pieces(values):
        high = values.astype(jnp.bfloat16)
        rest = values - high.astype(jnp.float32)
        middle = rest.astype(jnp.bfloat16)
        low = (rest - middle.astype(jnp.float32)).astype(jnp.bfloat16)
        return [high, middle, low]

    def body(i, totals):
        start = pl.multiple_of(i * 8, 8)
        ids = ids_ref[pl.ds(start, 8), :]
        upper = both_ref[pl.ds(start, 8), pl.ds(0, 128)]
        lower = both_ref[pl.ds(start, 8), pl.ds(128, 128)]
        hots, parts = [], []
        for j in range(8):
            cell = ids[j : j + 1, :]
            hots.append((jnp.bitwise_and(cell, 127) == lanes).astype(jnp.bfloat16))
            on_level = jnp.right_shift(cell, 7) == levels
            rows = jnp.concatenate(
                [
                    jnp.where(on_level, upper[j : j + 1, :], 0.0),
                    jnp.where(on_level, lower[j : j + 1, :], 0.0),
                ],
                axis=0,
            )
            parts.append(jnp.concatenate(pieces(rows), axis=0))
        added = lax.dot_general(
            jnp.concatenate(parts, axis=1),
            jnp.concatenate(hots, axis=1),
            (((1,), (1,)), ((), ())),
            preferred_element_type=jnp.float32,
        )
        return totals + added

    totals = lax.fori_loop(
        0, tiles, body, jnp.zeros((6 * map_rows, 128), jnp.float32), unroll=True
    )
    span = 2 * map_rows
    out_ref[...] = (totals[:span] + totals[span : 2 * span]) + totals[2 * span :]


def scatter_cells(local_map, both, map_rows):
    return pl.pallas_call(
        scatter_kernel,
        out_shape=jax.ShapeDtypeStruct((2 * map_rows, 128), jnp.float32),
        in_specs=[pl.BlockSpec(memory_space=pltpu.VMEM)] * 2,
        out_specs=pl.BlockSpec(memory_space=pltpu.VMEM),
    )(local_map, both)


def segregation(saturation, retention, gravity):
    burden = gravity * saturation * (1.0 - saturation)
    zero_plane = jnp.zeros(saturation.shape[1:], jnp.float32)
    local_end, _ = lax.scan(descend, zero_plane, (retention, burden))
    through = jnp.prod(retention, axis=0)
    depth_size = lax.axis_size("gz")
    pair = jnp.stack([through, local_end])
    behind = [from_behind(pair, "gz", d) for d in range(1, depth_size)]
    entering = zero_plane
    for d in range(depth_size - 1, 0, -1):
        above = behind[d - 1]
        entering = above[0] * entering + above[1]
    _, inflow = lax.scan(descend, entering, (retention, burden))
    return inflow, burden


def on_device(saturation, retention, gravity, cell_map, owner_id, stream_dir, node_weight, flight):
    layers, rows_x, rows_y = saturation.shape
    size_x = lax.axis_size("gx")
    size_y = lax.axis_size("gy")
    groups = size_x * size_y
    seg_len = cell_map.shape[2]
    capacity = cell_map.shape[1] // groups
    flat = saturation.reshape(-1)
    cell_count = flat.shape[0]
    map_rows = min(cell_count // 128, max(8, capacity * seg_len // 32))
    local_map = cell_map[0]

    offered = gather_cells(saturation, local_map, map_rows)
    arrived = lax.all_to_all(offered, ("gx", "gy"), split_axis=0, concat_axis=0, tiled=True)
    owners = owner_id[0, :, 0]
    rows = slot_rows(owners, groups, capacity)
    node_in = arrived[rows]
    seg_dev = node_in.shape[0]
    updated = transport(
        node_in.reshape(seg_dev // 2, 2 * seg_len),
        flight[0].reshape(seg_dev // 2, 2 * seg_len),
        stream_dir[0],
    )
    updated = updated.reshape(seg_dev, seg_len)
    weights = node_weight[0]
    slots = groups * capacity
    filled = rows[None, :] == jnp.arange(slots, dtype=jnp.int32)[:, None]
    source = jnp.sum(jnp.where(filled, jnp.arange(seg_dev, dtype=jnp.int32)[None, :], 0), axis=1)
    used = jnp.any(filled, axis=1)
    joined = jnp.concatenate([weights * updated, weights], axis=1)
    joined = jnp.concatenate([joined, jnp.zeros((1, 2 * seg_len), jnp.float32)], axis=0)
    package = joined[jnp.where(used, source, seg_dev)]
    returned = lax.all_to_all(package, ("gx", "gy"), split_axis=0, concat_axis=0, tiled=True)
    package, retention, gravity = lax.optimization_barrier((package, retention, gravity))
    inflow, burden = segregation(saturation, retention, gravity)
    sums = scatter_cells(local_map, returned, map_rows)
    padding = jnp.zeros((cell_count - map_rows * 128,), jnp.float32)
    numerator = jnp.concatenate([sums[:map_rows].reshape(-1), padding])
    denominator = jnp.concatenate([sums[map_rows:].reshape(-1), padding])
    mixed = ((flat + numerator) / (1.0 + denominator)).reshape(layers, rows_x, rows_y)
    final_sat = mixed + inflow - burden
    return (final_sat, updated[None])


def solution(mesh):
    return jax.shard_map(
        on_device,
        mesh=mesh,
        in_specs=(
            P("gz", "gx", "gy"),
            P("gz", "gx", "gy"),
            P("gz", "gx", "gy"),
            P("gz", ("gx", "gy"), None),
            P("gz", ("gx", "gy"), None),
            P("gz", ("gx", "gy")),
            P("gz", ("gx", "gy"), None),
            P("gz", ("gx", "gy"), None),
        ),
        out_specs=(P("gz", "gx", "gy"), P("gz", ("gx", "gy"), None)),
        check_vma=False,
    )
```

```python
import jax
import jax.numpy as jnp
from jax import lax
from jax.experimental import pallas as pl
from jax.experimental.pallas import tpu as pltpu
from jax.sharding import PartitionSpec as P


BL_STEPS = 8


def from_behind(block, axis, distance):
    devices = range(lax.axis_size(axis))
    route = [(i - distance, i) for i in devices if i - distance in devices]
    return lax.ppermute(block, axis, route)


def frac_flow(values):
    return values * values / (values * values + (1.0 - values) * (1.0 - values))


def transport(node_sat, increments, reversed_flag):
    flipped = reversed_flag[..., None] == 1
    state = jnp.where(flipped, node_sat[..., ::-1], node_sat)
    ratio = jnp.where(flipped, increments[..., ::-1], increments)
    inlet = jnp.ones(state.shape[:-1] + (1,), jnp.float32)
    for _ in range(BL_STEPS):
        flows = frac_flow(state)
        upstream = jnp.concatenate([inlet, flows[..., :-1]], axis=-1)
        state = state - ratio * (flows - upstream)
    return jnp.where(flipped, state[..., ::-1], state)


def slot_rows(owners, groups, capacity):
    onehot = (owners[:, None] == jnp.arange(groups, dtype=jnp.int32)[None, :]).astype(jnp.int32)
    before = jnp.cumsum(onehot, axis=0) - onehot
    return owners * capacity + jnp.sum(before * onehot, axis=1)


def descend(carried, layer):
    keep, drop = layer
    inflow = keep * carried
    return (inflow + drop, inflow)


def gather_kernel(table_ref, ids_ref, out_ref):
    map_rows = table_ref.shape[1]
    tiles = ids_ref.shape[0] // 8
    table = table_ref[0]
    spread = [jnp.broadcast_to(table[r : r + 1, :], (8, 128)) for r in range(map_rows)]

    def body(i, carry):
        start = pl.multiple_of(i * 8, 8)
        ids = ids_ref[pl.ds(start, 8), :]
        lane = jnp.bitwise_and(ids, 127)
        level = jnp.right_shift(ids, 7)
        picked = jnp.zeros((8, 128), jnp.float32)
        for r in range(map_rows):
            got = jnp.take_along_axis(spread[r], lane, axis=1, mode="promise_in_bounds")
            picked = jnp.where(level == r, got, picked)
        out_ref[pl.ds(start, 8), :] = picked
        return carry

    lax.fori_loop(0, tiles, body, 0, unroll=True)


def gather_cells(saturation, local_map, map_rows):
    return pl.pallas_call(
        gather_kernel,
        out_shape=jax.ShapeDtypeStruct(local_map.shape, jnp.float32),
        grid=(1,),
        in_specs=[
            pl.BlockSpec((1, map_rows, 128), lambda i: (0, 0, 0)),
            pl.BlockSpec(local_map.shape, lambda i: (0, 0)),
        ],
        out_specs=pl.BlockSpec(local_map.shape, lambda i: (0, 0)),
    )(saturation, local_map)


def scatter_kernel(ids_ref, both_ref, out_ref):
    map_rows = out_ref.shape[0] // 2
    tiles = ids_ref.shape[0] // 8
    lanes = lax.broadcasted_iota(jnp.int32, (128, 128), 0)
    levels = lax.broadcasted_iota(jnp.int32, (map_rows, 128), 0)

    def pieces(values):
        high = values.astype(jnp.bfloat16)
        rest = values - high.astype(jnp.float32)
        middle = rest.astype(jnp.bfloat16)
        low = (rest - middle.astype(jnp.float32)).astype(jnp.bfloat16)
        return [high, middle, low]

    def body(i, totals):
        start = pl.multiple_of(i * 8, 8)
        ids = ids_ref[pl.ds(start, 8), :]
        upper = both_ref[pl.ds(2 * start, 8, stride=2), :]
        lower = both_ref[pl.ds(2 * start + 1, 8, stride=2), :]
        hots, parts = [], []
        for j in range(8):
            cell = ids[j : j + 1, :]
            hots.append((jnp.bitwise_and(cell, 127) == lanes).astype(jnp.bfloat16))
            on_level = jnp.right_shift(cell, 7) == levels
            rows = jnp.concatenate(
                [
                    jnp.where(on_level, upper[j : j + 1, :], 0.0),
                    jnp.where(on_level, lower[j : j + 1, :], 0.0),
                ],
                axis=0,
            )
            parts.append(jnp.concatenate(pieces(rows), axis=0))
        added = lax.dot_general(
            jnp.concatenate(parts, axis=1),
            jnp.concatenate(hots, axis=1),
            (((1,), (1,)), ((), ())),
            preferred_element_type=jnp.float32,
        )
        return totals + added

    totals = lax.fori_loop(
        0, tiles, body, jnp.zeros((6 * map_rows, 128), jnp.float32), unroll=True
    )
    span = 2 * map_rows
    out_ref[...] = (totals[:span] + totals[span : 2 * span]) + totals[2 * span :]


def scatter_cells(local_map, both, map_rows):
    return pl.pallas_call(
        scatter_kernel,
        out_shape=jax.ShapeDtypeStruct((2 * map_rows, 128), jnp.float32),
        in_specs=[pl.BlockSpec(memory_space=pltpu.VMEM)] * 2,
        out_specs=pl.BlockSpec(memory_space=pltpu.VMEM),
    )(local_map, both)


def segregation(saturation, retention, gravity):
    burden = gravity * saturation * (1.0 - saturation)
    zero_plane = jnp.zeros(saturation.shape[1:], jnp.float32)
    local_end, _ = lax.scan(descend, zero_plane, (retention, burden))
    through = jnp.prod(retention, axis=0)
    depth_size = lax.axis_size("gz")
    pair = jnp.stack([through, local_end])
    behind = [from_behind(pair, "gz", d) for d in range(1, depth_size)]
    entering = zero_plane
    for d in range(depth_size - 1, 0, -1):
        above = behind[d - 1]
        entering = above[0] * entering + above[1]
    _, inflow = lax.scan(descend, entering, (retention, burden))
    return inflow, burden


def on_device(saturation, retention, gravity, cell_map, owner_id, stream_dir, node_weight, flight):
    layers, rows_x, rows_y = saturation.shape
    size_x = lax.axis_size("gx")
    size_y = lax.axis_size("gy")
    groups = size_x * size_y
    seg_len = cell_map.shape[2]
    capacity = cell_map.shape[1] // groups
    flat = saturation.reshape(-1)
    cell_count = flat.shape[0]
    map_rows = min(cell_count // 128, max(8, capacity * seg_len // 32))
    local_map = cell_map[0]

    offered = gather_cells(saturation, local_map, map_rows)
    arrived = lax.all_to_all(offered, ("gx", "gy"), split_axis=0, concat_axis=0, tiled=True)
    owners = owner_id[0, :, 0]
    rows = slot_rows(owners, groups, capacity)
    node_in = arrived[rows]
    seg_dev = node_in.shape[0]
    updated = transport(
        node_in.reshape(seg_dev // 2, 2 * seg_len),
        flight[0].reshape(seg_dev // 2, 2 * seg_len),
        stream_dir[0],
    )
    updated = updated.reshape(seg_dev, seg_len)
    weights = node_weight[0]
    slots = groups * capacity
    filled = rows[None, :] == jnp.arange(slots, dtype=jnp.int32)[:, None]
    source = jnp.sum(jnp.where(filled, jnp.arange(seg_dev, dtype=jnp.int32)[None, :], 0), axis=1)
    used = jnp.any(filled, axis=1)
    joined = jnp.concatenate(
        [weights * updated, weights, jnp.zeros((1, seg_len), jnp.float32)], axis=0
    )
    picks = jnp.stack([source, source + seg_dev], axis=1)
    package = joined[jnp.where(used[:, None], picks, 2 * seg_dev).reshape(-1)]
    returned = lax.all_to_all(package, ("gx", "gy"), split_axis=0, concat_axis=0, tiled=True)
    package, retention, gravity = lax.optimization_barrier((package, retention, gravity))
    inflow, burden = segregation(saturation, retention, gravity)
    sums = scatter_cells(local_map, returned, map_rows)
    padding = jnp.zeros((cell_count - map_rows * 128,), jnp.float32)
    numerator = jnp.concatenate([sums[:map_rows].reshape(-1), padding])
    denominator = jnp.concatenate([sums[map_rows:].reshape(-1), padding])
    mixed = ((flat + numerator) / (1.0 + denominator)).reshape(layers, rows_x, rows_y)
    final_sat = mixed + inflow - burden
    return (final_sat, updated[None])


def solution(mesh):
    return jax.shard_map(
        on_device,
        mesh=mesh,
        in_specs=(
            P("gz", "gx", "gy"),
            P("gz", "gx", "gy"),
            P("gz", "gx", "gy"),
            P("gz", ("gx", "gy"), None),
            P("gz", ("gx", "gy"), None),
            P("gz", ("gx", "gy")),
            P("gz", ("gx", "gy"), None),
            P("gz", ("gx", "gy"), None),
        ),
        out_specs=(P("gz", "gx", "gy"), P("gz", ("gx", "gy"), None)),
        check_vma=False,
    )
```

```python
import jax
import jax.numpy as jnp
from jax import lax
from jax.experimental import pallas as pl
from jax.experimental.pallas import tpu as pltpu
from jax.sharding import PartitionSpec as P


BL_STEPS = 8


def from_behind(block, axis, distance):
    devices = range(lax.axis_size(axis))
    route = [(i - distance, i) for i in devices if i - distance in devices]
    return lax.ppermute(block, axis, route)


def frac_flow(values):
    return values * values / (values * values + (1.0 - values) * (1.0 - values))


def transport(node_sat, increments, reversed_flag):
    flipped = reversed_flag[..., None] == 1
    state = jnp.where(flipped, node_sat[..., ::-1], node_sat)
    ratio = jnp.where(flipped, increments[..., ::-1], increments)
    inlet = jnp.ones(state.shape[:-1] + (1,), jnp.float32)
    for _ in range(BL_STEPS):
        flows = frac_flow(state)
        upstream = jnp.concatenate([inlet, flows[..., :-1]], axis=-1)
        state = state - ratio * (flows - upstream)
    return jnp.where(flipped, state[..., ::-1], state)


def slot_rows(owners, groups, capacity):
    onehot = (owners[:, None] == jnp.arange(groups, dtype=jnp.int32)[None, :]).astype(jnp.int32)
    before = jnp.cumsum(onehot, axis=0) - onehot
    return owners * capacity + jnp.sum(before * onehot, axis=1)


def descend(carried, layer):
    keep, drop = layer
    inflow = keep * carried
    return (inflow + drop, inflow)


def gather_kernel(table_ref, ids_ref, out_ref):
    map_rows = table_ref.shape[1]
    tiles = ids_ref.shape[0] // 8
    table = table_ref[0]
    spread = [jnp.broadcast_to(table[r : r + 1, :], (8, 128)) for r in range(map_rows)]

    def body(i, carry):
        start = pl.multiple_of(i * 8, 8)
        ids = ids_ref[pl.ds(start, 8), :]
        lane = jnp.bitwise_and(ids, 127)
        level = jnp.right_shift(ids, 7)
        picked = jnp.zeros((8, 128), jnp.float32)
        for r in range(map_rows):
            got = jnp.take_along_axis(spread[r], lane, axis=1, mode="promise_in_bounds")
            picked = jnp.where(level == r, got, picked)
        out_ref[pl.ds(start, 8), :] = picked
        return carry

    lax.fori_loop(0, tiles, body, 0, unroll=True)


def gather_cells(saturation, local_map, map_rows):
    return pl.pallas_call(
        gather_kernel,
        out_shape=jax.ShapeDtypeStruct(local_map.shape, jnp.float32),
        grid=(1,),
        in_specs=[
            pl.BlockSpec((1, map_rows, 128), lambda i: (0, 0, 0)),
            pl.BlockSpec(local_map.shape, lambda i: (0, 0)),
        ],
        out_specs=pl.BlockSpec(local_map.shape, lambda i: (0, 0)),
    )(saturation, local_map)


def scatter_kernel(ids_ref, both_ref, out_ref):
    map_rows = out_ref.shape[1]
    tiles = ids_ref.shape[0] // 8
    lanes = lax.broadcasted_iota(jnp.int32, (128, 128), 0)
    levels = lax.broadcasted_iota(jnp.int32, (map_rows, 128), 0)

    def pieces(values):
        high = values.astype(jnp.bfloat16)
        rest = values - high.astype(jnp.float32)
        middle = rest.astype(jnp.bfloat16)
        low = (rest - middle.astype(jnp.float32)).astype(jnp.bfloat16)
        return [high, middle, low]

    def body(i, totals):
        start = pl.multiple_of(i * 8, 8)
        ids = ids_ref[pl.ds(start, 8), :]
        upper = both_ref[pl.ds(2 * start, 8, stride=2), :]
        lower = both_ref[pl.ds(2 * start + 1, 8, stride=2), :]
        hots, parts = [], []
        for j in range(8):
            cell = ids[j : j + 1, :]
            hots.append((jnp.bitwise_and(cell, 127) == lanes).astype(jnp.bfloat16))
            on_level = jnp.right_shift(cell, 7) == levels
            rows = jnp.concatenate(
                [
                    jnp.where(on_level, upper[j : j + 1, :], 0.0),
                    jnp.where(on_level, lower[j : j + 1, :], 0.0),
                ],
                axis=0,
            )
            parts.append(jnp.concatenate(pieces(rows), axis=0))
        added = lax.dot_general(
            jnp.concatenate(parts, axis=1),
            jnp.concatenate(hots, axis=1),
            (((1,), (1,)), ((), ())),
            preferred_element_type=jnp.float32,
        )
        return totals + added

    totals = lax.fori_loop(
        0, tiles, body, jnp.zeros((6 * map_rows, 128), jnp.float32), unroll=True
    )
    span = 2 * map_rows
    summed = (totals[:span] + totals[span : 2 * span]) + totals[2 * span :]
    out_ref[0] = summed[:map_rows]
    out_ref[1] = summed[map_rows:]


def scatter_cells(local_map, both, map_rows):
    return pl.pallas_call(
        scatter_kernel,
        out_shape=jax.ShapeDtypeStruct((2, map_rows, 128), jnp.float32),
        in_specs=[pl.BlockSpec(memory_space=pltpu.VMEM)] * 2,
        out_specs=pl.BlockSpec(memory_space=pltpu.VMEM),
    )(local_map, both)


def segregation(saturation, retention, gravity):
    burden = gravity * saturation * (1.0 - saturation)
    zero_plane = jnp.zeros(saturation.shape[1:], jnp.float32)
    local_end, _ = lax.scan(descend, zero_plane, (retention, burden))
    through = jnp.prod(retention, axis=0)
    depth_size = lax.axis_size("gz")
    pair = jnp.stack([through, local_end])
    behind = [from_behind(pair, "gz", d) for d in range(1, depth_size)]
    entering = zero_plane
    for d in range(depth_size - 1, 0, -1):
        above = behind[d - 1]
        entering = above[0] * entering + above[1]
    _, inflow = lax.scan(descend, entering, (retention, burden))
    return inflow, burden


def on_device(saturation, retention, gravity, cell_map, owner_id, stream_dir, node_weight, flight):
    layers, rows_x, rows_y = saturation.shape
    size_x = lax.axis_size("gx")
    size_y = lax.axis_size("gy")
    groups = size_x * size_y
    seg_len = cell_map.shape[2]
    capacity = cell_map.shape[1] // groups
    flat = saturation.reshape(-1)
    cell_count = flat.shape[0]
    map_rows = min(cell_count // 128, max(8, capacity * seg_len // 32))
    local_map = cell_map[0]

    offered = gather_cells(saturation, local_map, map_rows)
    arrived = lax.all_to_all(offered, ("gx", "gy"), split_axis=0, concat_axis=0, tiled=True)
    owners = owner_id[0, :, 0]
    rows = slot_rows(owners, groups, capacity)
    node_in = arrived[rows]
    seg_dev = node_in.shape[0]
    updated = transport(
        node_in.reshape(seg_dev // 2, 2 * seg_len),
        flight[0].reshape(seg_dev // 2, 2 * seg_len),
        stream_dir[0],
    )
    updated = updated.reshape(seg_dev, seg_len)
    weights = node_weight[0]
    slots = groups * capacity
    filled = rows[None, :] == jnp.arange(slots, dtype=jnp.int32)[:, None]
    source = jnp.sum(jnp.where(filled, jnp.arange(seg_dev, dtype=jnp.int32)[None, :], 0), axis=1)
    used = jnp.any(filled, axis=1)
    joined = jnp.concatenate(
        [weights * updated, weights, jnp.zeros((1, seg_len), jnp.float32)], axis=0
    )
    picks = jnp.stack([source, source + seg_dev], axis=1)
    package = joined[jnp.where(used[:, None], picks, 2 * seg_dev).reshape(-1)]
    returned = lax.all_to_all(package, ("gx", "gy"), split_axis=0, concat_axis=0, tiled=True)
    package, retention, gravity = lax.optimization_barrier((package, retention, gravity))
    inflow, burden = segregation(saturation, retention, gravity)
    sums = scatter_cells(local_map, returned, map_rows)
    head_rows = (map_rows * 128) // rows_y
    cover = ((0, layers - 1), (0, rows_x - head_rows), (0, 0))
    numerator = jnp.pad(sums[0].reshape(1, head_rows, rows_y), cover)
    denominator = jnp.pad(sums[1].reshape(1, head_rows, rows_y), cover)
    mixed = (saturation + numerator) / (1.0 + denominator)
    final_sat = mixed + inflow - burden
    return (final_sat, updated[None])


def solution(mesh):
    return jax.shard_map(
        on_device,
        mesh=mesh,
        in_specs=(
            P("gz", "gx", "gy"),
            P("gz", "gx", "gy"),
            P("gz", "gx", "gy"),
            P("gz", ("gx", "gy"), None),
            P("gz", ("gx", "gy"), None),
            P("gz", ("gx", "gy")),
            P("gz", ("gx", "gy"), None),
            P("gz", ("gx", "gy"), None),
        ),
        out_specs=(P("gz", "gx", "gy"), P("gz", ("gx", "gy"), None)),
        check_vma=False,
    )
```

```python
import jax
import jax.numpy as jnp
from jax import lax
from jax.experimental import pallas as pl
from jax.experimental.pallas import tpu as pltpu
from jax.sharding import PartitionSpec as P


BL_STEPS = 8


def from_behind(block, axis, distance):
    devices = range(lax.axis_size(axis))
    route = [(i - distance, i) for i in devices if i - distance in devices]
    return lax.ppermute(block, axis, route)


def frac_flow(values):
    return values * values / (values * values + (1.0 - values) * (1.0 - values))


def transport(node_sat, increments, reversed_flag):
    flipped = reversed_flag[..., None] == 1
    state = node_sat
    inlet = jnp.ones(state.shape[:-1] + (1,), jnp.float32)
    for _ in range(BL_STEPS):
        flows = frac_flow(state)
        from_left = jnp.concatenate([inlet, flows[..., :-1]], axis=-1)
        from_right = jnp.concatenate([flows[..., 1:], inlet], axis=-1)
        upstream = jnp.where(flipped, from_right, from_left)
        state = state - increments * (flows - upstream)
    return state


def slot_rows(owners, groups, capacity):
    onehot = (owners[:, None] == jnp.arange(groups, dtype=jnp.int32)[None, :]).astype(jnp.int32)
    before = jnp.cumsum(onehot, axis=0) - onehot
    return owners * capacity + jnp.sum(before * onehot, axis=1)


def descend(carried, layer):
    keep, drop = layer
    inflow = keep * carried
    return (inflow + drop, inflow)


def gather_kernel(table_ref, ids_ref, out_ref):
    map_rows = table_ref.shape[1]
    tiles = ids_ref.shape[0] // 8
    table = table_ref[0]
    spread = [jnp.broadcast_to(table[r : r + 1, :], (8, 128)) for r in range(map_rows)]

    def body(i, carry):
        start = pl.multiple_of(i * 8, 8)
        ids = ids_ref[pl.ds(start, 8), :]
        lane = jnp.bitwise_and(ids, 127)
        level = jnp.right_shift(ids, 7)
        picked = jnp.zeros((8, 128), jnp.float32)
        for r in range(map_rows):
            got = jnp.take_along_axis(spread[r], lane, axis=1, mode="promise_in_bounds")
            picked = jnp.where(level == r, got, picked)
        out_ref[pl.ds(start, 8), :] = picked
        return carry

    lax.fori_loop(0, tiles, body, 0, unroll=True)


def gather_cells(saturation, local_map, map_rows):
    return pl.pallas_call(
        gather_kernel,
        out_shape=jax.ShapeDtypeStruct(local_map.shape, jnp.float32),
        grid=(1,),
        in_specs=[
            pl.BlockSpec((1, map_rows, 128), lambda i: (0, 0, 0)),
            pl.BlockSpec(local_map.shape, lambda i: (0, 0)),
        ],
        out_specs=pl.BlockSpec(local_map.shape, lambda i: (0, 0)),
    )(saturation, local_map)


def scatter_kernel(ids_ref, both_ref, out_ref):
    map_rows = out_ref.shape[1]
    tiles = ids_ref.shape[0] // 8
    lanes = lax.broadcasted_iota(jnp.int32, (128, 128), 0)
    levels = lax.broadcasted_iota(jnp.int32, (map_rows, 128), 0)

    def pieces(values):
        high = values.astype(jnp.bfloat16)
        rest = values - high.astype(jnp.float32)
        middle = rest.astype(jnp.bfloat16)
        low = (rest - middle.astype(jnp.float32)).astype(jnp.bfloat16)
        return [high, middle, low]

    def body(i, totals):
        start = pl.multiple_of(i * 8, 8)
        ids = ids_ref[pl.ds(start, 8), :]
        upper = both_ref[pl.ds(2 * start, 8, stride=2), :]
        lower = both_ref[pl.ds(2 * start + 1, 8, stride=2), :]
        hots, parts = [], []
        for j in range(8):
            cell = ids[j : j + 1, :]
            hots.append((jnp.bitwise_and(cell, 127) == lanes).astype(jnp.bfloat16))
            on_level = jnp.right_shift(cell, 7) == levels
            rows = jnp.concatenate(
                [
                    jnp.where(on_level, upper[j : j + 1, :], 0.0),
                    jnp.where(on_level, lower[j : j + 1, :], 0.0),
                ],
                axis=0,
            )
            parts.append(jnp.concatenate(pieces(rows), axis=0))
        added = lax.dot_general(
            jnp.concatenate(parts, axis=1),
            jnp.concatenate(hots, axis=1),
            (((1,), (1,)), ((), ())),
            preferred_element_type=jnp.float32,
        )
        return totals + added

    totals = lax.fori_loop(
        0, tiles, body, jnp.zeros((6 * map_rows, 128), jnp.float32), unroll=True
    )
    span = 2 * map_rows
    summed = (totals[:span] + totals[span : 2 * span]) + totals[2 * span :]
    out_ref[0] = summed[:map_rows]
    out_ref[1] = summed[map_rows:]


def scatter_cells(local_map, both, map_rows):
    return pl.pallas_call(
        scatter_kernel,
        out_shape=jax.ShapeDtypeStruct((2, map_rows, 128), jnp.float32),
        in_specs=[pl.BlockSpec(memory_space=pltpu.VMEM)] * 2,
        out_specs=pl.BlockSpec(memory_space=pltpu.VMEM),
    )(local_map, both)


def segregation(saturation, retention, gravity):
    burden = gravity * saturation * (1.0 - saturation)
    zero_plane = jnp.zeros(saturation.shape[1:], jnp.float32)
    local_end, _ = lax.scan(descend, zero_plane, (retention, burden))
    through = jnp.prod(retention, axis=0)
    depth_size = lax.axis_size("gz")
    pair = jnp.stack([through, local_end])
    behind = [from_behind(pair, "gz", d) for d in range(1, depth_size)]
    entering = zero_plane
    for d in range(depth_size - 1, 0, -1):
        above = behind[d - 1]
        entering = above[0] * entering + above[1]
    _, inflow = lax.scan(descend, entering, (retention, burden))
    return inflow, burden


def on_device(saturation, retention, gravity, cell_map, owner_id, stream_dir, node_weight, flight):
    layers, rows_x, rows_y = saturation.shape
    size_x = lax.axis_size("gx")
    size_y = lax.axis_size("gy")
    groups = size_x * size_y
    seg_len = cell_map.shape[2]
    capacity = cell_map.shape[1] // groups
    flat = saturation.reshape(-1)
    cell_count = flat.shape[0]
    map_rows = min(cell_count // 128, max(8, capacity * seg_len // 32))
    local_map = cell_map[0]

    offered = gather_cells(saturation, local_map, map_rows)
    arrived = lax.all_to_all(offered, ("gx", "gy"), split_axis=0, concat_axis=0, tiled=True)
    owners = owner_id[0, :, 0]
    rows = slot_rows(owners, groups, capacity)
    node_in = arrived[rows]
    seg_dev = node_in.shape[0]
    updated = transport(
        node_in.reshape(seg_dev // 2, 2 * seg_len),
        flight[0].reshape(seg_dev // 2, 2 * seg_len),
        stream_dir[0],
    )
    updated = updated.reshape(seg_dev, seg_len)
    weights = node_weight[0]
    slots = groups * capacity
    filled = rows[None, :] == jnp.arange(slots, dtype=jnp.int32)[:, None]
    source = jnp.sum(jnp.where(filled, jnp.arange(seg_dev, dtype=jnp.int32)[None, :], 0), axis=1)
    used = jnp.any(filled, axis=1)
    joined = jnp.concatenate(
        [weights * updated, weights, jnp.zeros((1, seg_len), jnp.float32)], axis=0
    )
    picks = jnp.stack([source, source + seg_dev], axis=1)
    package = joined[jnp.where(used[:, None], picks, 2 * seg_dev).reshape(-1)]
    returned = lax.all_to_all(package, ("gx", "gy"), split_axis=0, concat_axis=0, tiled=True)
    package, retention, gravity = lax.optimization_barrier((package, retention, gravity))
    inflow, burden = segregation(saturation, retention, gravity)
    sums = scatter_cells(local_map, returned, map_rows)
    head_rows = (map_rows * 128) // rows_y
    cover = ((0, layers - 1), (0, rows_x - head_rows), (0, 0))
    numerator = jnp.pad(sums[0].reshape(1, head_rows, rows_y), cover)
    denominator = jnp.pad(sums[1].reshape(1, head_rows, rows_y), cover)
    mixed = (saturation + numerator) / (1.0 + denominator)
    final_sat = mixed + inflow - burden
    return (final_sat, updated[None])


def solution(mesh):
    return jax.shard_map(
        on_device,
        mesh=mesh,
        in_specs=(
            P("gz", "gx", "gy"),
            P("gz", "gx", "gy"),
            P("gz", "gx", "gy"),
            P("gz", ("gx", "gy"), None),
            P("gz", ("gx", "gy"), None),
            P("gz", ("gx", "gy")),
            P("gz", ("gx", "gy"), None),
            P("gz", ("gx", "gy"), None),
        ),
        out_specs=(P("gz", "gx", "gy"), P("gz", ("gx", "gy"), None)),
        check_vma=False,
    )
```

```python
import jax
import jax.numpy as jnp
from jax import lax
from jax.experimental import pallas as pl
from jax.experimental.pallas import tpu as pltpu
from jax.sharding import PartitionSpec as P


BL_STEPS = 8


def from_behind(block, axis, distance):
    devices = range(lax.axis_size(axis))
    route = [(i - distance, i) for i in devices if i - distance in devices]
    return lax.ppermute(block, axis, route)


def frac_flow(values):
    return values * values / (values * values + (1.0 - values) * (1.0 - values))


def transport(node_sat, increments, reversed_flag):
    flipped = reversed_flag[..., None] == 1
    state = node_sat
    inlet = jnp.ones(state.shape[:-1] + (1,), jnp.float32)
    for _ in range(BL_STEPS):
        flows = frac_flow(state)
        from_left = jnp.concatenate([inlet, flows[..., :-1]], axis=-1)
        from_right = jnp.concatenate([flows[..., 1:], inlet], axis=-1)
        upstream = jnp.where(flipped, from_right, from_left)
        state = state - increments * (flows - upstream)
    return state


def slot_rows(owners, groups, capacity):
    onehot = (owners[:, None] == jnp.arange(groups, dtype=jnp.int32)[None, :]).astype(jnp.int32)
    before = jnp.cumsum(onehot, axis=0) - onehot
    return owners * capacity + jnp.sum(before * onehot, axis=1)


def descend(carried, layer):
    keep, drop = layer
    inflow = keep * carried
    return (inflow + drop, inflow)


def gather_kernel(table_ref, ids_ref, out_ref):
    map_rows = table_ref.shape[1]
    tiles = ids_ref.shape[0] // 8
    table = table_ref[0]
    spread = [jnp.broadcast_to(table[r : r + 1, :], (8, 128)) for r in range(map_rows)]

    def body(i, carry):
        start = pl.multiple_of(i * 8, 8)
        ids = ids_ref[pl.ds(start, 8), :]
        lane = jnp.bitwise_and(ids, 127)
        level = jnp.right_shift(ids, 7)
        picked = jnp.zeros((8, 128), jnp.float32)
        for r in range(map_rows):
            got = jnp.take_along_axis(spread[r], lane, axis=1, mode="promise_in_bounds")
            picked = jnp.where(level == r, got, picked)
        out_ref[pl.ds(start, 8), :] = picked
        return carry

    lax.fori_loop(0, tiles, body, 0, unroll=True)


def gather_cells(saturation, local_map, map_rows):
    return pl.pallas_call(
        gather_kernel,
        out_shape=jax.ShapeDtypeStruct(local_map.shape, jnp.float32),
        grid=(1,),
        in_specs=[
            pl.BlockSpec((1, map_rows, 128), lambda i: (0, 0, 0)),
            pl.BlockSpec(local_map.shape, lambda i: (0, 0)),
        ],
        out_specs=pl.BlockSpec(local_map.shape, lambda i: (0, 0)),
    )(saturation, local_map)


def scatter_kernel(ids_ref, both_ref, out_ref):
    map_rows = out_ref.shape[1]
    tiles = ids_ref.shape[0] // 8
    lanes = lax.broadcasted_iota(jnp.int32, (128, 128), 0)
    levels = lax.broadcasted_iota(jnp.int32, (map_rows, 128), 0)

    def pieces(values):
        high = values.astype(jnp.bfloat16)
        rest = values - high.astype(jnp.float32)
        middle = rest.astype(jnp.bfloat16)
        low = (rest - middle.astype(jnp.float32)).astype(jnp.bfloat16)
        return [high, middle, low]

    def body(i, totals):
        start = pl.multiple_of(i * 8, 8)
        ids = ids_ref[pl.ds(start, 8), :]
        upper = both_ref[pl.ds(2 * start, 8, stride=2), :]
        lower = both_ref[pl.ds(2 * start + 1, 8, stride=2), :]
        hots, parts = [], []
        for j in range(8):
            cell = ids[j : j + 1, :]
            hots.append((jnp.bitwise_and(cell, 127) == lanes).astype(jnp.bfloat16))
            on_level = jnp.right_shift(cell, 7) == levels
            rows = jnp.concatenate(
                [
                    jnp.where(on_level, upper[j : j + 1, :], 0.0),
                    jnp.where(on_level, lower[j : j + 1, :], 0.0),
                ],
                axis=0,
            )
            parts.append(jnp.concatenate(pieces(rows), axis=0))
        added = lax.dot_general(
            jnp.concatenate(parts, axis=1),
            jnp.concatenate(hots, axis=1),
            (((1,), (1,)), ((), ())),
            preferred_element_type=jnp.float32,
        )
        return totals + added

    totals = lax.fori_loop(
        0, tiles, body, jnp.zeros((6 * map_rows, 128), jnp.float32), unroll=True
    )
    span = 2 * map_rows
    summed = (totals[:span] + totals[span : 2 * span]) + totals[2 * span :]
    out_ref[0] = summed[:map_rows]
    out_ref[1] = summed[map_rows:]


def scatter_cells(local_map, both, map_rows):
    return pl.pallas_call(
        scatter_kernel,
        out_shape=jax.ShapeDtypeStruct((2, map_rows, 128), jnp.float32),
        in_specs=[pl.BlockSpec(memory_space=pltpu.VMEM)] * 2,
        out_specs=pl.BlockSpec(memory_space=pltpu.VMEM),
    )(local_map, both)


def segregation(saturation, retention, gravity):
    burden = gravity * saturation * (1.0 - saturation)
    zero_plane = jnp.zeros(saturation.shape[1:], jnp.float32)
    local_end, _ = lax.scan(descend, zero_plane, (retention, burden))
    through = jnp.prod(retention, axis=0)
    depth_size = lax.axis_size("gz")
    pair = jnp.stack([through, local_end])
    behind = [from_behind(pair, "gz", d) for d in range(1, depth_size)]
    entering = zero_plane
    for d in range(depth_size - 1, 0, -1):
        above = behind[d - 1]
        entering = above[0] * entering + above[1]
    _, inflow = lax.scan(descend, entering, (retention, burden))
    return inflow, burden


def on_device(saturation, retention, gravity, cell_map, owner_id, stream_dir, node_weight, flight):
    layers, rows_x, rows_y = saturation.shape
    size_x = lax.axis_size("gx")
    size_y = lax.axis_size("gy")
    groups = size_x * size_y
    seg_len = cell_map.shape[2]
    capacity = cell_map.shape[1] // groups
    flat = saturation.reshape(-1)
    cell_count = flat.shape[0]
    map_rows = min(cell_count // 128, max(8, capacity * seg_len // 32))
    local_map = cell_map[0]

    offered = gather_cells(saturation, local_map, map_rows)
    arrived = lax.all_to_all(offered, ("gx", "gy"), split_axis=0, concat_axis=0, tiled=True)
    owners = owner_id[0, :, 0]
    rows = slot_rows(owners, groups, capacity)
    slots = groups * capacity
    filled = rows[None, :] == jnp.arange(slots, dtype=jnp.int32)[:, None]
    node_in = jnp.dot(
        filled.T.astype(jnp.float32),
        arrived,
        precision=lax.Precision.HIGHEST,
        preferred_element_type=jnp.float32,
    )
    seg_dev = node_in.shape[0]
    updated = transport(
        node_in.reshape(seg_dev // 2, 2 * seg_len),
        flight[0].reshape(seg_dev // 2, 2 * seg_len),
        stream_dir[0],
    )
    updated = updated.reshape(seg_dev, seg_len)
    weights = node_weight[0]
    joined = jnp.concatenate([weights * updated, weights], axis=0)
    halves = jnp.arange(2, dtype=jnp.int32)
    spread = (filled[:, None, None, :] & (halves[None, :, None, None] == halves[None, None, :, None]))
    package = jnp.dot(
        spread.reshape(2 * slots, 2 * seg_dev).astype(jnp.float32),
        joined,
        precision=lax.Precision.HIGHEST,
        preferred_element_type=jnp.float32,
    )
    returned = lax.all_to_all(package, ("gx", "gy"), split_axis=0, concat_axis=0, tiled=True)
    package, retention, gravity = lax.optimization_barrier((package, retention, gravity))
    inflow, burden = segregation(saturation, retention, gravity)
    sums = scatter_cells(local_map, returned, map_rows)
    head_rows = (map_rows * 128) // rows_y
    cover = ((0, layers - 1), (0, rows_x - head_rows), (0, 0))
    numerator = jnp.pad(sums[0].reshape(1, head_rows, rows_y), cover)
    denominator = jnp.pad(sums[1].reshape(1, head_rows, rows_y), cover)
    mixed = (saturation + numerator) / (1.0 + denominator)
    final_sat = mixed + inflow - burden
    return (final_sat, updated[None])


def solution(mesh):
    return jax.shard_map(
        on_device,
        mesh=mesh,
        in_specs=(
            P("gz", "gx", "gy"),
            P("gz", "gx", "gy"),
            P("gz", "gx", "gy"),
            P("gz", ("gx", "gy"), None),
            P("gz", ("gx", "gy"), None),
            P("gz", ("gx", "gy")),
            P("gz", ("gx", "gy"), None),
            P("gz", ("gx", "gy"), None),
        ),
        out_specs=(P("gz", "gx", "gy"), P("gz", ("gx", "gy"), None)),
        check_vma=False,
    )
```

```python
import jax
import jax.numpy as jnp
from jax import lax
from jax.experimental import pallas as pl
from jax.experimental.pallas import tpu as pltpu
from jax.sharding import PartitionSpec as P


BL_STEPS = 8


def from_behind(block, axis, distance):
    devices = range(lax.axis_size(axis))
    route = [(i - distance, i) for i in devices if i - distance in devices]
    return lax.ppermute(block, axis, route)


def frac_flow(values):
    return values * values / (values * values + (1.0 - values) * (1.0 - values))


def transport(node_sat, increments, reversed_flag):
    flipped = reversed_flag[..., None] == 1
    state = node_sat
    inlet = jnp.ones(state.shape[:-1] + (1,), jnp.float32)
    for _ in range(BL_STEPS):
        flows = frac_flow(state)
        from_left = jnp.concatenate([inlet, flows[..., :-1]], axis=-1)
        from_right = jnp.concatenate([flows[..., 1:], inlet], axis=-1)
        upstream = jnp.where(flipped, from_right, from_left)
        state = state - increments * (flows - upstream)
    return state


def slot_rows(owners, groups, capacity):
    onehot = (owners[:, None] == jnp.arange(groups, dtype=jnp.int32)[None, :]).astype(jnp.int32)
    before = jnp.cumsum(onehot, axis=0) - onehot
    return owners * capacity + jnp.sum(before * onehot, axis=1)


def descend(carried, layer):
    keep, drop = layer
    inflow = keep * carried
    return (inflow + drop, inflow)


def gather_kernel(table_ref, ids_ref, out_ref):
    map_rows = table_ref.shape[1]
    tiles = ids_ref.shape[0] // 8
    table = table_ref[0]
    spread = [jnp.broadcast_to(table[r : r + 1, :], (8, 128)) for r in range(map_rows)]

    def body(i, carry):
        start = pl.multiple_of(i * 8, 8)
        ids = ids_ref[pl.ds(start, 8), :]
        lane = jnp.bitwise_and(ids, 127)
        level = jnp.right_shift(ids, 7)
        picked = jnp.zeros((8, 128), jnp.float32)
        for r in range(map_rows):
            got = jnp.take_along_axis(spread[r], lane, axis=1, mode="promise_in_bounds")
            picked = jnp.where(level == r, got, picked)
        out_ref[pl.ds(start, 8), :] = picked
        return carry

    lax.fori_loop(0, tiles, body, 0, unroll=True)


def gather_cells(saturation, local_map, map_rows):
    return pl.pallas_call(
        gather_kernel,
        out_shape=jax.ShapeDtypeStruct(local_map.shape, jnp.float32),
        grid=(1,),
        in_specs=[
            pl.BlockSpec((1, map_rows, 128), lambda i: (0, 0, 0)),
            pl.BlockSpec(local_map.shape, lambda i: (0, 0)),
        ],
        out_specs=pl.BlockSpec(local_map.shape, lambda i: (0, 0)),
    )(saturation, local_map)


def scatter_kernel(ids_ref, both_ref, out_ref):
    map_rows = out_ref.shape[1]
    tiles = ids_ref.shape[0] // 8
    lanes = lax.broadcasted_iota(jnp.int32, (128, 128), 0)
    levels = lax.broadcasted_iota(jnp.int32, (map_rows, 128), 0)

    def pieces(values):
        high = values.astype(jnp.bfloat16)
        rest = values - high.astype(jnp.float32)
        middle = rest.astype(jnp.bfloat16)
        low = (rest - middle.astype(jnp.float32)).astype(jnp.bfloat16)
        return [high, middle, low]

    def body(i, totals):
        start = pl.multiple_of(i * 8, 8)
        ids = ids_ref[pl.ds(start, 8), :]
        upper = both_ref[pl.ds(2 * start, 8, stride=2), :]
        lower = both_ref[pl.ds(2 * start + 1, 8, stride=2), :]
        hots, parts = [], []
        for j in range(8):
            cell = ids[j : j + 1, :]
            hots.append((jnp.bitwise_and(cell, 127) == lanes).astype(jnp.bfloat16))
            on_level = jnp.right_shift(cell, 7) == levels
            rows = jnp.concatenate(
                [
                    jnp.where(on_level, upper[j : j + 1, :], 0.0),
                    jnp.where(on_level, lower[j : j + 1, :], 0.0),
                ],
                axis=0,
            )
            parts.append(jnp.concatenate(pieces(rows), axis=0))
        added = lax.dot_general(
            jnp.concatenate(parts, axis=1),
            jnp.concatenate(hots, axis=1),
            (((1,), (1,)), ((), ())),
            preferred_element_type=jnp.float32,
        )
        return totals + added

    totals = lax.fori_loop(
        0, tiles, body, jnp.zeros((6 * map_rows, 128), jnp.float32), unroll=True
    )
    span = 2 * map_rows
    summed = (totals[:span] + totals[span : 2 * span]) + totals[2 * span :]
    out_ref[0] = summed[:map_rows]
    out_ref[1] = summed[map_rows:]


def scatter_cells(local_map, both, map_rows):
    return pl.pallas_call(
        scatter_kernel,
        out_shape=jax.ShapeDtypeStruct((2, map_rows, 128), jnp.float32),
        in_specs=[pl.BlockSpec(memory_space=pltpu.VMEM)] * 2,
        out_specs=pl.BlockSpec(memory_space=pltpu.VMEM),
    )(local_map, both)


def segregation(saturation, retention, gravity):
    burden = gravity * saturation * (1.0 - saturation)
    zero_plane = jnp.zeros(saturation.shape[1:], jnp.float32)
    local_end, _ = lax.scan(descend, zero_plane, (retention, burden))
    through = jnp.prod(retention, axis=0)
    depth_size = lax.axis_size("gz")
    pair = jnp.stack([through, local_end])
    behind = [from_behind(pair, "gz", d) for d in range(1, depth_size)]
    entering = zero_plane
    for d in range(depth_size - 1, 0, -1):
        above = behind[d - 1]
        entering = above[0] * entering + above[1]
    _, inflow = lax.scan(descend, entering, (retention, burden))
    return inflow, burden


def on_device(saturation, retention, gravity, cell_map, owner_id, stream_dir, node_weight, flight):
    layers, rows_x, rows_y = saturation.shape
    size_x = lax.axis_size("gx")
    size_y = lax.axis_size("gy")
    groups = size_x * size_y
    seg_len = cell_map.shape[2]
    capacity = cell_map.shape[1] // groups
    flat = saturation.reshape(-1)
    cell_count = flat.shape[0]
    map_rows = min(cell_count // 128, max(8, capacity * seg_len // 32))
    local_map = cell_map[0]

    offered = gather_cells(saturation, local_map, map_rows)
    arrived = lax.all_to_all(offered, ("gx", "gy"), split_axis=0, concat_axis=0, tiled=True)
    owners = owner_id[0, :, 0]
    rows = slot_rows(owners, groups, capacity)
    slots = groups * capacity
    filled = rows[None, :] == jnp.arange(slots, dtype=jnp.int32)[:, None]
    segments = rows.shape[0]
    weights = node_weight[0]
    halves = lax.broadcasted_iota(jnp.int32, (slots, 2, segments), 1)
    sat_rows = (filled[:, None, :] & (halves == 0)).reshape(2 * slots, segments)
    weight_rows = (filled[:, None, :] & (halves == 1)).reshape(2 * slots, segments)
    weight_part = jnp.dot(
        weight_rows.astype(jnp.float32),
        weights,
        precision=lax.Precision.HIGHEST,
        preferred_element_type=jnp.float32,
    )
    weight_part, arrived = lax.optimization_barrier((weight_part, arrived))
    node_in = jnp.dot(
        filled.T.astype(jnp.float32),
        arrived,
        precision=lax.Precision.HIGHEST,
        preferred_element_type=jnp.float32,
    )
    seg_dev = node_in.shape[0]
    updated = transport(
        node_in.reshape(seg_dev // 2, 2 * seg_len),
        flight[0].reshape(seg_dev // 2, 2 * seg_len),
        stream_dir[0],
    )
    updated = updated.reshape(seg_dev, seg_len)
    package = weight_part + jnp.dot(
        sat_rows.astype(jnp.float32),
        weights * updated,
        precision=lax.Precision.HIGHEST,
        preferred_element_type=jnp.float32,
    )
    returned = lax.all_to_all(package, ("gx", "gy"), split_axis=0, concat_axis=0, tiled=True)
    package, retention, gravity = lax.optimization_barrier((package, retention, gravity))
    inflow, burden = segregation(saturation, retention, gravity)
    sums = scatter_cells(local_map, returned, map_rows)
    head_rows = (map_rows * 128) // rows_y
    cover = ((0, layers - 1), (0, rows_x - head_rows), (0, 0))
    numerator = jnp.pad(sums[0].reshape(1, head_rows, rows_y), cover)
    denominator = jnp.pad(sums[1].reshape(1, head_rows, rows_y), cover)
    mixed = (saturation + numerator) / (1.0 + denominator)
    final_sat = mixed + inflow - burden
    return (final_sat, updated[None])


def solution(mesh):
    return jax.shard_map(
        on_device,
        mesh=mesh,
        in_specs=(
            P("gz", "gx", "gy"),
            P("gz", "gx", "gy"),
            P("gz", "gx", "gy"),
            P("gz", ("gx", "gy"), None),
            P("gz", ("gx", "gy"), None),
            P("gz", ("gx", "gy")),
            P("gz", ("gx", "gy"), None),
            P("gz", ("gx", "gy"), None),
        ),
        out_specs=(P("gz", "gx", "gy"), P("gz", ("gx", "gy"), None)),
        check_vma=False,
    )
```

```python
import jax
import jax.numpy as jnp
from jax import lax
from jax.experimental import pallas as pl
from jax.experimental.pallas import tpu as pltpu
from jax.sharding import PartitionSpec as P


BL_STEPS = 8


def from_behind(block, axis, distance):
    devices = range(lax.axis_size(axis))
    route = [(i - distance, i) for i in devices if i - distance in devices]
    return lax.ppermute(block, axis, route)


def frac_flow(values):
    return values * values / (values * values + (1.0 - values) * (1.0 - values))


def slot_rows(owners, groups, capacity):
    onehot = (owners[:, None] == jnp.arange(groups, dtype=jnp.int32)[None, :]).astype(jnp.int32)
    before = jnp.cumsum(onehot, axis=0) - onehot
    return owners * capacity + jnp.sum(before * onehot, axis=1)


def descend(carried, layer):
    keep, drop = layer
    inflow = keep * carried
    return (inflow + drop, inflow)


def transport_kernel(state_ref, ratio_ref, flag_ref, out_ref):
    state = state_ref[...]
    ratio = ratio_ref[...]
    flipped = flag_ref[...] == 1
    width = state.shape[1]
    lane = lax.broadcasted_iota(jnp.int32, state.shape, 1)
    for _ in range(BL_STEPS):
        flows = frac_flow(state)
        from_left = jnp.where(lane == 0, 1.0, pltpu.roll(flows, 1, axis=1))
        from_right = jnp.where(lane == width - 1, 1.0, pltpu.roll(flows, width - 1, axis=1))
        upstream = jnp.where(flipped, from_right, from_left)
        state = state - ratio * (flows - upstream)
    out_ref[...] = state


def transport_lines(node_sat, increments, reversed_flag):
    return pl.pallas_call(
        transport_kernel,
        out_shape=jax.ShapeDtypeStruct(node_sat.shape, jnp.float32),
        in_specs=[pl.BlockSpec(memory_space=pltpu.VMEM)] * 3,
        out_specs=pl.BlockSpec(memory_space=pltpu.VMEM),
    )(node_sat, increments, reversed_flag[:, None])


def gather_kernel(table_ref, ids_ref, out_ref):
    map_rows = table_ref.shape[1]
    tiles = ids_ref.shape[0] // 8
    table = table_ref[0]
    spread = [jnp.broadcast_to(table[r : r + 1, :], (8, 128)) for r in range(map_rows)]

    def body(i, carry):
        start = pl.multiple_of(i * 8, 8)
        ids = ids_ref[pl.ds(start, 8), :]
        lane = jnp.bitwise_and(ids, 127)
        level = jnp.right_shift(ids, 7)
        picked = jnp.zeros((8, 128), jnp.float32)
        for r in range(map_rows):
            got = jnp.take_along_axis(spread[r], lane, axis=1, mode="promise_in_bounds")
            picked = jnp.where(level == r, got, picked)
        out_ref[pl.ds(start, 8), :] = picked
        return carry

    lax.fori_loop(0, tiles, body, 0, unroll=True)


def gather_cells(saturation, local_map, map_rows):
    return pl.pallas_call(
        gather_kernel,
        out_shape=jax.ShapeDtypeStruct(local_map.shape, jnp.float32),
        grid=(1,),
        in_specs=[
            pl.BlockSpec((1, map_rows, 128), lambda i: (0, 0, 0)),
            pl.BlockSpec(local_map.shape, lambda i: (0, 0)),
        ],
        out_specs=pl.BlockSpec(local_map.shape, lambda i: (0, 0)),
    )(saturation, local_map)


def scatter_kernel(ids_ref, both_ref, out_ref):
    map_rows = out_ref.shape[1]
    tiles = ids_ref.shape[0] // 8
    lanes = lax.broadcasted_iota(jnp.int32, (128, 128), 0)
    levels = lax.broadcasted_iota(jnp.int32, (map_rows, 128), 0)

    def pieces(values):
        high = values.astype(jnp.bfloat16)
        rest = values - high.astype(jnp.float32)
        middle = rest.astype(jnp.bfloat16)
        low = (rest - middle.astype(jnp.float32)).astype(jnp.bfloat16)
        return [high, middle, low]

    def body(i, totals):
        start = pl.multiple_of(i * 8, 8)
        ids = ids_ref[pl.ds(start, 8), :]
        upper = both_ref[pl.ds(2 * start, 8, stride=2), :]
        lower = both_ref[pl.ds(2 * start + 1, 8, stride=2), :]
        hots, parts = [], []
        for j in range(8):
            cell = ids[j : j + 1, :]
            hots.append((jnp.bitwise_and(cell, 127) == lanes).astype(jnp.bfloat16))
            on_level = jnp.right_shift(cell, 7) == levels
            rows = jnp.concatenate(
                [
                    jnp.where(on_level, upper[j : j + 1, :], 0.0),
                    jnp.where(on_level, lower[j : j + 1, :], 0.0),
                ],
                axis=0,
            )
            parts.append(jnp.concatenate(pieces(rows), axis=0))
        added = lax.dot_general(
            jnp.concatenate(parts, axis=1),
            jnp.concatenate(hots, axis=1),
            (((1,), (1,)), ((), ())),
            preferred_element_type=jnp.float32,
        )
        return totals + added

    totals = lax.fori_loop(
        0, tiles, body, jnp.zeros((6 * map_rows, 128), jnp.float32), unroll=True
    )
    span = 2 * map_rows
    summed = (totals[:span] + totals[span : 2 * span]) + totals[2 * span :]
    out_ref[0] = summed[:map_rows]
    out_ref[1] = summed[map_rows:]


def scatter_cells(local_map, both, map_rows):
    return pl.pallas_call(
        scatter_kernel,
        out_shape=jax.ShapeDtypeStruct((2, map_rows, 128), jnp.float32),
        in_specs=[pl.BlockSpec(memory_space=pltpu.VMEM)] * 2,
        out_specs=pl.BlockSpec(memory_space=pltpu.VMEM),
    )(local_map, both)


def segregation(saturation, retention, gravity):
    burden = gravity * saturation * (1.0 - saturation)
    zero_plane = jnp.zeros(saturation.shape[1:], jnp.float32)
    local_end, _ = lax.scan(descend, zero_plane, (retention, burden))
    through = jnp.prod(retention, axis=0)
    depth_size = lax.axis_size("gz")
    pair = jnp.stack([through, local_end])
    behind = [from_behind(pair, "gz", d) for d in range(1, depth_size)]
    entering = zero_plane
    for d in range(depth_size - 1, 0, -1):
        above = behind[d - 1]
        entering = above[0] * entering + above[1]
    _, inflow = lax.scan(descend, entering, (retention, burden))
    return inflow, burden


def on_device(saturation, retention, gravity, cell_map, owner_id, stream_dir, node_weight, flight):
    layers, rows_x, rows_y = saturation.shape
    size_x = lax.axis_size("gx")
    size_y = lax.axis_size("gy")
    groups = size_x * size_y
    seg_len = cell_map.shape[2]
    capacity = cell_map.shape[1] // groups
    flat = saturation.reshape(-1)
    cell_count = flat.shape[0]
    map_rows = min(cell_count // 128, max(8, capacity * seg_len // 32))
    local_map = cell_map[0]

    offered = gather_cells(saturation, local_map, map_rows)
    arrived = lax.all_to_all(offered, ("gx", "gy"), split_axis=0, concat_axis=0, tiled=True)
    owners = owner_id[0, :, 0]
    rows = slot_rows(owners, groups, capacity)
    slots = groups * capacity
    filled = rows[None, :] == jnp.arange(slots, dtype=jnp.int32)[:, None]
    segments = rows.shape[0]
    weights = node_weight[0]
    halves = lax.broadcasted_iota(jnp.int32, (slots, 2, segments), 1)
    sat_rows = (filled[:, None, :] & (halves == 0)).reshape(2 * slots, segments)
    weight_rows = (filled[:, None, :] & (halves == 1)).reshape(2 * slots, segments)
    weight_part = jnp.dot(
        weight_rows.astype(jnp.float32),
        weights,
        precision=lax.Precision.HIGHEST,
        preferred_element_type=jnp.float32,
    )
    weight_part, arrived = lax.optimization_barrier((weight_part, arrived))
    node_in = jnp.dot(
        filled.T.astype(jnp.float32),
        arrived,
        precision=lax.Precision.HIGHEST,
        preferred_element_type=jnp.float32,
    )
    seg_dev = node_in.shape[0]
    updated = transport_lines(
        node_in.reshape(seg_dev // 2, 2 * seg_len),
        flight[0].reshape(seg_dev // 2, 2 * seg_len),
        stream_dir[0],
    )
    updated = updated.reshape(seg_dev, seg_len)
    package = weight_part + jnp.dot(
        sat_rows.astype(jnp.float32),
        weights * updated,
        precision=lax.Precision.HIGHEST,
        preferred_element_type=jnp.float32,
    )
    returned = lax.all_to_all(package, ("gx", "gy"), split_axis=0, concat_axis=0, tiled=True)
    package, retention, gravity = lax.optimization_barrier((package, retention, gravity))
    inflow, burden = segregation(saturation, retention, gravity)
    sums = scatter_cells(local_map, returned, map_rows)
    head_rows = (map_rows * 128) // rows_y
    cover = ((0, layers - 1), (0, rows_x - head_rows), (0, 0))
    numerator = jnp.pad(sums[0].reshape(1, head_rows, rows_y), cover)
    denominator = jnp.pad(sums[1].reshape(1, head_rows, rows_y), cover)
    mixed = (saturation + numerator) / (1.0 + denominator)
    final_sat = mixed + inflow - burden
    return (final_sat, updated[None])


def solution(mesh):
    return jax.shard_map(
        on_device,
        mesh=mesh,
        in_specs=(
            P("gz", "gx", "gy"),
            P("gz", "gx", "gy"),
            P("gz", "gx", "gy"),
            P("gz", ("gx", "gy"), None),
            P("gz", ("gx", "gy"), None),
            P("gz", ("gx", "gy")),
            P("gz", ("gx", "gy"), None),
            P("gz", ("gx", "gy"), None),
        ),
        out_specs=(P("gz", "gx", "gy"), P("gz", ("gx", "gy"), None)),
        check_vma=False,
    )
```

```python
import functools

import jax
import jax.numpy as jnp
from jax import lax
from jax.experimental import pallas as pl
from jax.experimental.pallas import tpu as pltpu
from jax.sharding import PartitionSpec as P


BL_STEPS = 8


def from_behind(block, axis, distance):
    devices = range(lax.axis_size(axis))
    route = [(i - distance, i) for i in devices if i - distance in devices]
    return lax.ppermute(block, axis, route)


def frac_flow(values):
    return values * values / (values * values + (1.0 - values) * (1.0 - values))


def transport(node_sat, increments, reversed_flag):
    flipped = reversed_flag[..., None] == 1
    state = node_sat
    inlet = jnp.ones(state.shape[:-1] + (1,), jnp.float32)
    for _ in range(BL_STEPS):
        flows = frac_flow(state)
        from_left = jnp.concatenate([inlet, flows[..., :-1]], axis=-1)
        from_right = jnp.concatenate([flows[..., 1:], inlet], axis=-1)
        upstream = jnp.where(flipped, from_right, from_left)
        state = state - increments * (flows - upstream)
    return state


def slot_rows(owners, groups, capacity):
    onehot = (owners[:, None] == jnp.arange(groups, dtype=jnp.int32)[None, :]).astype(jnp.int32)
    before = jnp.cumsum(onehot, axis=0) - onehot
    return owners * capacity + jnp.sum(before * onehot, axis=1)


def descend(carried, layer):
    keep, drop = layer
    inflow = keep * carried
    return (inflow + drop, inflow)


def gather_kernel(table_ref, ids_ref, out_ref):
    map_rows = table_ref.shape[1]
    tiles = ids_ref.shape[0] // 8
    table = table_ref[0]
    spread = [jnp.broadcast_to(table[r : r + 1, :], (8, 128)) for r in range(map_rows)]

    def body(i, carry):
        start = pl.multiple_of(i * 8, 8)
        ids = ids_ref[pl.ds(start, 8), :]
        lane = jnp.bitwise_and(ids, 127)
        level = jnp.right_shift(ids, 7)
        picked = jnp.zeros((8, 128), jnp.float32)
        for r in range(map_rows):
            got = jnp.take_along_axis(spread[r], lane, axis=1, mode="promise_in_bounds")
            picked = jnp.where(level == r, got, picked)
        out_ref[pl.ds(start, 8), :] = picked
        return carry

    lax.fori_loop(0, tiles, body, 0, unroll=True)


def gather_cells(saturation, local_map, map_rows):
    return pl.pallas_call(
        gather_kernel,
        out_shape=jax.ShapeDtypeStruct(local_map.shape, jnp.float32),
        grid=(1,),
        in_specs=[
            pl.BlockSpec((1, map_rows, 128), lambda i: (0, 0, 0)),
            pl.BlockSpec(local_map.shape, lambda i: (0, 0)),
        ],
        out_specs=pl.BlockSpec(local_map.shape, lambda i: (0, 0)),
    )(saturation, local_map)


def scatter_kernel(map_rows, ids_ref, both_ref, sat_ref, inflow_ref, burden_ref, out_ref):
    tiles = ids_ref.shape[0] // 8
    lanes = lax.broadcasted_iota(jnp.int32, (128, 128), 0)
    levels = lax.broadcasted_iota(jnp.int32, (map_rows, 128), 0)

    def pieces(values):
        high = values.astype(jnp.bfloat16)
        rest = values - high.astype(jnp.float32)
        middle = rest.astype(jnp.bfloat16)
        low = (rest - middle.astype(jnp.float32)).astype(jnp.bfloat16)
        return [high, middle, low]

    def body(i, totals):
        start = pl.multiple_of(i * 8, 8)
        ids = ids_ref[pl.ds(start, 8), :]
        upper = both_ref[pl.ds(2 * start, 8, stride=2), :]
        lower = both_ref[pl.ds(2 * start + 1, 8, stride=2), :]
        hots, parts = [], []
        for j in range(8):
            cell = ids[j : j + 1, :]
            hots.append((jnp.bitwise_and(cell, 127) == lanes).astype(jnp.bfloat16))
            on_level = jnp.right_shift(cell, 7) == levels
            rows = jnp.concatenate(
                [
                    jnp.where(on_level, upper[j : j + 1, :], 0.0),
                    jnp.where(on_level, lower[j : j + 1, :], 0.0),
                ],
                axis=0,
            )
            parts.append(jnp.concatenate(pieces(rows), axis=0))
        added = lax.dot_general(
            jnp.concatenate(parts, axis=1),
            jnp.concatenate(hots, axis=1),
            (((1,), (1,)), ((), ())),
            preferred_element_type=jnp.float32,
        )
        return totals + added

    totals = lax.fori_loop(
        0, tiles, body, jnp.zeros((6 * map_rows, 128), jnp.float32), unroll=True
    )
    span = 2 * map_rows
    summed = (totals[:span] + totals[span : 2 * span]) + totals[2 * span :]
    out_ref[...] = (sat_ref[...] + inflow_ref[...]) - burden_ref[...]
    mixed = (sat_ref[0, :map_rows, :] + summed[:map_rows]) / (1.0 + summed[map_rows:])
    out_ref[0, :map_rows, :] = (mixed + inflow_ref[0, :map_rows, :]) - burden_ref[0, :map_rows, :]


def scatter_cells(local_map, both, saturation, inflow, burden, map_rows):
    return pl.pallas_call(
        functools.partial(scatter_kernel, map_rows),
        out_shape=jax.ShapeDtypeStruct(saturation.shape, jnp.float32),
        in_specs=[pl.BlockSpec(memory_space=pltpu.VMEM)] * 5,
        out_specs=pl.BlockSpec(memory_space=pltpu.VMEM),
    )(local_map, both, saturation, inflow, burden)


def segregation(saturation, retention, gravity):
    burden = gravity * saturation * (1.0 - saturation)
    zero_plane = jnp.zeros(saturation.shape[1:], jnp.float32)
    local_end, _ = lax.scan(descend, zero_plane, (retention, burden))
    through = jnp.prod(retention, axis=0)
    depth_size = lax.axis_size("gz")
    pair = jnp.stack([through, local_end])
    behind = [from_behind(pair, "gz", d) for d in range(1, depth_size)]
    entering = zero_plane
    for d in range(depth_size - 1, 0, -1):
        above = behind[d - 1]
        entering = above[0] * entering + above[1]
    _, inflow = lax.scan(descend, entering, (retention, burden))
    return inflow, burden


def on_device(saturation, retention, gravity, cell_map, owner_id, stream_dir, node_weight, flight):
    size_x = lax.axis_size("gx")
    size_y = lax.axis_size("gy")
    groups = size_x * size_y
    seg_len = cell_map.shape[2]
    capacity = cell_map.shape[1] // groups
    flat = saturation.reshape(-1)
    cell_count = flat.shape[0]
    map_rows = min(cell_count // 128, max(8, capacity * seg_len // 32))
    local_map = cell_map[0]

    offered = gather_cells(saturation, local_map, map_rows)
    arrived = lax.all_to_all(offered, ("gx", "gy"), split_axis=0, concat_axis=0, tiled=True)
    owners = owner_id[0, :, 0]
    rows = slot_rows(owners, groups, capacity)
    slots = groups * capacity
    filled = rows[None, :] == jnp.arange(slots, dtype=jnp.int32)[:, None]
    segments = rows.shape[0]
    weights = node_weight[0]
    halves = lax.broadcasted_iota(jnp.int32, (slots, 2, segments), 1)
    sat_rows = (filled[:, None, :] & (halves == 0)).reshape(2 * slots, segments)
    weight_rows = (filled[:, None, :] & (halves == 1)).reshape(2 * slots, segments)
    weight_part = jnp.dot(
        weight_rows.astype(jnp.float32),
        weights,
        precision=lax.Precision.HIGHEST,
        preferred_element_type=jnp.float32,
    )
    weight_part, arrived = lax.optimization_barrier((weight_part, arrived))
    node_in = jnp.dot(
        filled.T.astype(jnp.float32),
        arrived,
        precision=lax.Precision.HIGHEST,
        preferred_element_type=jnp.float32,
    )
    seg_dev = node_in.shape[0]
    updated = transport(
        node_in.reshape(seg_dev // 2, 2 * seg_len),
        flight[0].reshape(seg_dev // 2, 2 * seg_len),
        stream_dir[0],
    )
    updated = updated.reshape(seg_dev, seg_len)
    package = weight_part + jnp.dot(
        sat_rows.astype(jnp.float32),
        weights * updated,
        precision=lax.Precision.HIGHEST,
        preferred_element_type=jnp.float32,
    )
    returned = lax.all_to_all(package, ("gx", "gy"), split_axis=0, concat_axis=0, tiled=True)
    package, retention, gravity = lax.optimization_barrier((package, retention, gravity))
    inflow, burden = segregation(saturation, retention, gravity)
    final_sat = scatter_cells(local_map, returned, saturation, inflow, burden, map_rows)
    return (final_sat, updated[None])


def solution(mesh):
    return jax.shard_map(
        on_device,
        mesh=mesh,
        in_specs=(
            P("gz", "gx", "gy"),
            P("gz", "gx", "gy"),
            P("gz", "gx", "gy"),
            P("gz", ("gx", "gy"), None),
            P("gz", ("gx", "gy"), None),
            P("gz", ("gx", "gy")),
            P("gz", ("gx", "gy"), None),
            P("gz", ("gx", "gy"), None),
        ),
        out_specs=(P("gz", "gx", "gy"), P("gz", ("gx", "gy"), None)),
        check_vma=False,
    )
```

```python
import functools

import jax
import jax.numpy as jnp
from jax import lax
from jax.experimental import pallas as pl
from jax.experimental.pallas import tpu as pltpu
from jax.sharding import PartitionSpec as P


BL_STEPS = 8


def from_behind(block, axis, distance):
    devices = range(lax.axis_size(axis))
    route = [(i - distance, i) for i in devices if i - distance in devices]
    return lax.ppermute(block, axis, route)


def frac_flow(values):
    return values * values / (values * values + (1.0 - values) * (1.0 - values))


def transport(node_sat, increments, reversed_flag):
    flipped = reversed_flag[..., None] == 1
    state = node_sat
    inlet = jnp.ones(state.shape[:-1] + (1,), jnp.float32)
    lane = lax.broadcasted_iota(jnp.int32, state.shape, state.ndim - 1)
    last = state.shape[-1] - 1
    for _ in range(BL_STEPS):
        flows = frac_flow(state)
        left = jnp.concatenate([inlet, state[..., :-1]], axis=-1)
        right = jnp.concatenate([state[..., 1:], inlet], axis=-1)
        neighbour = jnp.where(flipped, right, left)
        edge = jnp.where(flipped, lane == last, lane == 0)
        upstream = jnp.where(edge, 1.0, frac_flow(neighbour))
        state = state - increments * (flows - upstream)
    return state


def slot_rows(owners, groups, capacity):
    onehot = (owners[:, None] == jnp.arange(groups, dtype=jnp.int32)[None, :]).astype(jnp.int32)
    before = jnp.cumsum(onehot, axis=0) - onehot
    return owners * capacity + jnp.sum(before * onehot, axis=1)


def descend(carried, layer):
    keep, drop = layer
    inflow = keep * carried
    return (inflow + drop, inflow)


def gather_kernel(table_ref, ids_ref, out_ref):
    map_rows = table_ref.shape[1]
    tiles = ids_ref.shape[0] // 8
    table = table_ref[0]
    spread = [jnp.broadcast_to(table[r : r + 1, :], (8, 128)) for r in range(map_rows)]

    def body(i, carry):
        start = pl.multiple_of(i * 8, 8)
        ids = ids_ref[pl.ds(start, 8), :]
        lane = jnp.bitwise_and(ids, 127)
        level = jnp.right_shift(ids, 7)
        picked = jnp.zeros((8, 128), jnp.float32)
        for r in range(map_rows):
            got = jnp.take_along_axis(spread[r], lane, axis=1, mode="promise_in_bounds")
            picked = jnp.where(level == r, got, picked)
        out_ref[pl.ds(start, 8), :] = picked
        return carry

    lax.fori_loop(0, tiles, body, 0, unroll=True)


def gather_cells(saturation, local_map, map_rows):
    return pl.pallas_call(
        gather_kernel,
        out_shape=jax.ShapeDtypeStruct(local_map.shape, jnp.float32),
        grid=(1,),
        in_specs=[
            pl.BlockSpec((1, map_rows, 128), lambda i: (0, 0, 0)),
            pl.BlockSpec(local_map.shape, lambda i: (0, 0)),
        ],
        out_specs=pl.BlockSpec(local_map.shape, lambda i: (0, 0)),
    )(saturation, local_map)


def scatter_kernel(map_rows, ids_ref, both_ref, sat_ref, inflow_ref, burden_ref, out_ref):
    tiles = ids_ref.shape[0] // 8
    lanes = lax.broadcasted_iota(jnp.int32, (128, 128), 0)
    levels = lax.broadcasted_iota(jnp.int32, (map_rows, 128), 0)

    def pieces(values):
        high = values.astype(jnp.bfloat16)
        rest = values - high.astype(jnp.float32)
        middle = rest.astype(jnp.bfloat16)
        low = (rest - middle.astype(jnp.float32)).astype(jnp.bfloat16)
        return [high, middle, low]

    def body(i, totals):
        start = pl.multiple_of(i * 8, 8)
        ids = ids_ref[pl.ds(start, 8), :]
        upper = both_ref[pl.ds(2 * start, 8, stride=2), :]
        lower = both_ref[pl.ds(2 * start + 1, 8, stride=2), :]
        hots, parts = [], []
        for j in range(8):
            cell = ids[j : j + 1, :]
            hots.append((jnp.bitwise_and(cell, 127) == lanes).astype(jnp.bfloat16))
            on_level = jnp.right_shift(cell, 7) == levels
            rows = jnp.concatenate(
                [
                    jnp.where(on_level, upper[j : j + 1, :], 0.0),
                    jnp.where(on_level, lower[j : j + 1, :], 0.0),
                ],
                axis=0,
            )
            parts.append(jnp.concatenate(pieces(rows), axis=0))
        added = lax.dot_general(
            jnp.concatenate(parts, axis=1),
            jnp.concatenate(hots, axis=1),
            (((1,), (1,)), ((), ())),
            preferred_element_type=jnp.float32,
        )
        return totals + added

    totals = lax.fori_loop(
        0, tiles, body, jnp.zeros((6 * map_rows, 128), jnp.float32), unroll=True
    )
    span = 2 * map_rows
    summed = (totals[:span] + totals[span : 2 * span]) + totals[2 * span :]
    out_ref[...] = (sat_ref[...] + inflow_ref[...]) - burden_ref[...]
    mixed = (sat_ref[0, :map_rows, :] + summed[:map_rows]) / (1.0 + summed[map_rows:])
    out_ref[0, :map_rows, :] = (mixed + inflow_ref[0, :map_rows, :]) - burden_ref[0, :map_rows, :]


def scatter_cells(local_map, both, saturation, inflow, burden, map_rows):
    return pl.pallas_call(
        functools.partial(scatter_kernel, map_rows),
        out_shape=jax.ShapeDtypeStruct(saturation.shape, jnp.float32),
        in_specs=[pl.BlockSpec(memory_space=pltpu.VMEM)] * 5,
        out_specs=pl.BlockSpec(memory_space=pltpu.VMEM),
    )(local_map, both, saturation, inflow, burden)


def segregation(saturation, retention, gravity):
    burden = gravity * saturation * (1.0 - saturation)
    zero_plane = jnp.zeros(saturation.shape[1:], jnp.float32)
    local_end, _ = lax.scan(descend, zero_plane, (retention, burden))
    through = jnp.prod(retention, axis=0)
    depth_size = lax.axis_size("gz")
    pair = jnp.stack([through, local_end])
    behind = [from_behind(pair, "gz", d) for d in range(1, depth_size)]
    entering = zero_plane
    for d in range(depth_size - 1, 0, -1):
        above = behind[d - 1]
        entering = above[0] * entering + above[1]
    _, inflow = lax.scan(descend, entering, (retention, burden))
    return inflow, burden


def on_device(saturation, retention, gravity, cell_map, owner_id, stream_dir, node_weight, flight):
    size_x = lax.axis_size("gx")
    size_y = lax.axis_size("gy")
    groups = size_x * size_y
    seg_len = cell_map.shape[2]
    capacity = cell_map.shape[1] // groups
    flat = saturation.reshape(-1)
    cell_count = flat.shape[0]
    map_rows = min(cell_count // 128, max(8, capacity * seg_len // 32))
    local_map = cell_map[0]

    offered = gather_cells(saturation, local_map, map_rows)
    arrived = lax.all_to_all(offered, ("gx", "gy"), split_axis=0, concat_axis=0, tiled=True)
    owners = owner_id[0, :, 0]
    rows = slot_rows(owners, groups, capacity)
    slots = groups * capacity
    filled = rows[None, :] == jnp.arange(slots, dtype=jnp.int32)[:, None]
    segments = rows.shape[0]
    weights = node_weight[0]
    halves = lax.broadcasted_iota(jnp.int32, (slots, 2, segments), 1)
    sat_rows = (filled[:, None, :] & (halves == 0)).reshape(2 * slots, segments)
    weight_rows = (filled[:, None, :] & (halves == 1)).reshape(2 * slots, segments)
    weight_part = jnp.dot(
        weight_rows.astype(jnp.float32),
        weights,
        precision=lax.Precision.HIGHEST,
        preferred_element_type=jnp.float32,
    )
    weight_part, arrived = lax.optimization_barrier((weight_part, arrived))
    node_in = jnp.dot(
        filled.T.astype(jnp.float32),
        arrived,
        precision=lax.Precision.HIGHEST,
        preferred_element_type=jnp.float32,
    )
    seg_dev = node_in.shape[0]
    updated = transport(
        node_in.reshape(seg_dev // 2, 2 * seg_len),
        flight[0].reshape(seg_dev // 2, 2 * seg_len),
        stream_dir[0],
    )
    updated = updated.reshape(seg_dev, seg_len)
    package = weight_part + jnp.dot(
        sat_rows.astype(jnp.float32),
        weights * updated,
        precision=lax.Precision.HIGHEST,
        preferred_element_type=jnp.float32,
    )
    returned = lax.all_to_all(package, ("gx", "gy"), split_axis=0, concat_axis=0, tiled=True)
    package, retention, gravity = lax.optimization_barrier((package, retention, gravity))
    inflow, burden = segregation(saturation, retention, gravity)
    final_sat = scatter_cells(local_map, returned, saturation, inflow, burden, map_rows)
    return (final_sat, updated[None])


def solution(mesh):
    return jax.shard_map(
        on_device,
        mesh=mesh,
        in_specs=(
            P("gz", "gx", "gy"),
            P("gz", "gx", "gy"),
            P("gz", "gx", "gy"),
            P("gz", ("gx", "gy"), None),
            P("gz", ("gx", "gy"), None),
            P("gz", ("gx", "gy")),
            P("gz", ("gx", "gy"), None),
            P("gz", ("gx", "gy"), None),
        ),
        out_specs=(P("gz", "gx", "gy"), P("gz", ("gx", "gy"), None)),
        check_vma=False,
    )
```

```python
import functools

import jax
import jax.numpy as jnp
from jax import lax
from jax.experimental import pallas as pl
from jax.experimental.pallas import tpu as pltpu
from jax.sharding import PartitionSpec as P


BL_STEPS = 8


def from_behind(block, axis, distance):
    devices = range(lax.axis_size(axis))
    route = [(i - distance, i) for i in devices if i - distance in devices]
    return lax.ppermute(block, axis, route)


def frac_flow(values):
    return values * values / (values * values + (1.0 - values) * (1.0 - values))


def transport(node_sat, increments, reversed_flag):
    flipped = reversed_flag[..., None] == 1
    state = node_sat
    inlet = jnp.ones(state.shape[:-1] + (1,), jnp.float32)
    for _ in range(BL_STEPS):
        flows = frac_flow(state)
        from_left = jnp.concatenate([inlet, flows[..., :-1]], axis=-1)
        from_right = jnp.concatenate([flows[..., 1:], inlet], axis=-1)
        upstream = jnp.where(flipped, from_right, from_left)
        state = state - increments * (flows - upstream)
    return state


def slot_rows(owners, groups, capacity):
    onehot = (owners[:, None] == jnp.arange(groups, dtype=jnp.int32)[None, :]).astype(jnp.int32)
    before = jnp.cumsum(onehot, axis=0) - onehot
    return owners * capacity + jnp.sum(before * onehot, axis=1)


def descend(carried, layer):
    keep, drop = layer
    inflow = keep * carried
    return (inflow + drop, inflow)


def gather_kernel(table_ref, ids_ref, out_ref):
    map_rows = table_ref.shape[1]
    tiles = ids_ref.shape[0] // 8
    table = table_ref[0]
    spread = [jnp.broadcast_to(table[r : r + 1, :], (8, 128)) for r in range(map_rows)]

    def body(i, carry):
        start = pl.multiple_of(i * 8, 8)
        ids = ids_ref[pl.ds(start, 8), :]
        lane = jnp.bitwise_and(ids, 127)
        level = jnp.right_shift(ids, 7)
        picked = jnp.zeros((8, 128), jnp.float32)
        for r in range(map_rows):
            got = jnp.take_along_axis(spread[r], lane, axis=1, mode="promise_in_bounds")
            picked = jnp.where(level == r, got, picked)
        out_ref[pl.ds(start, 8), :] = picked
        return carry

    lax.fori_loop(0, tiles, body, 0, unroll=True)


def gather_cells(saturation, local_map, map_rows):
    return pl.pallas_call(
        gather_kernel,
        out_shape=jax.ShapeDtypeStruct(local_map.shape, jnp.float32),
        grid=(1,),
        in_specs=[
            pl.BlockSpec((1, map_rows, 128), lambda i: (0, 0, 0)),
            pl.BlockSpec(local_map.shape, lambda i: (0, 0)),
        ],
        out_specs=pl.BlockSpec(local_map.shape, lambda i: (0, 0)),
    )(saturation, local_map)


def scatter_kernel(map_rows, ids_ref, hots_ref, both_ref, sat_ref, inflow_ref, burden_ref, out_ref):
    tiles = ids_ref.shape[0] // 8
    lanes = lax.broadcasted_iota(jnp.int32, (128, 128), 0)
    levels = lax.broadcasted_iota(jnp.int32, (map_rows, 128), 0)

    def pieces(values):
        high = values.astype(jnp.bfloat16)
        rest = values - high.astype(jnp.float32)
        middle = rest.astype(jnp.bfloat16)
        low = (rest - middle.astype(jnp.float32)).astype(jnp.bfloat16)
        return [high, middle, low]

    def body(i, totals):
        start = pl.multiple_of(i * 8, 8)
        ids = ids_ref[pl.ds(start, 8), :]
        upper = both_ref[pl.ds(2 * start, 8, stride=2), :]
        lower = both_ref[pl.ds(2 * start + 1, 8, stride=2), :]
        hots, parts = [], []
        for j in range(8):
            cell = ids[j : j + 1, :]
            hots.append(hots_ref[start + j])
            on_level = jnp.right_shift(cell, 7) == levels
            rows = jnp.concatenate(
                [
                    jnp.where(on_level, upper[j : j + 1, :], 0.0),
                    jnp.where(on_level, lower[j : j + 1, :], 0.0),
                ],
                axis=0,
            )
            parts.append(jnp.concatenate(pieces(rows), axis=0))
        added = lax.dot_general(
            jnp.concatenate(parts, axis=1),
            jnp.concatenate(hots, axis=1),
            (((1,), (1,)), ((), ())),
            preferred_element_type=jnp.float32,
        )
        return totals + added

    totals = lax.fori_loop(
        0, tiles, body, jnp.zeros((6 * map_rows, 128), jnp.float32), unroll=True
    )
    span = 2 * map_rows
    summed = (totals[:span] + totals[span : 2 * span]) + totals[2 * span :]
    out_ref[...] = (sat_ref[...] + inflow_ref[...]) - burden_ref[...]
    mixed = (sat_ref[0, :map_rows, :] + summed[:map_rows]) / (1.0 + summed[map_rows:])
    out_ref[0, :map_rows, :] = (mixed + inflow_ref[0, :map_rows, :]) - burden_ref[0, :map_rows, :]


def scatter_cells(local_map, both, saturation, inflow, burden, map_rows):
    lanes = lax.broadcasted_iota(jnp.int32, (1, 128, 1), 1)
    hots = (jnp.bitwise_and(local_map, 127)[:, None, :] == lanes).astype(jnp.bfloat16)
    return pl.pallas_call(
        functools.partial(scatter_kernel, map_rows),
        out_shape=jax.ShapeDtypeStruct(saturation.shape, jnp.float32),
        in_specs=[pl.BlockSpec(memory_space=pltpu.VMEM)] * 6,
        out_specs=pl.BlockSpec(memory_space=pltpu.VMEM),
        compiler_params=pltpu.CompilerParams(vmem_limit_bytes=40 * 1024 * 1024),
    )(local_map, hots, both, saturation, inflow, burden)


def segregation(saturation, retention, gravity):
    burden = gravity * saturation * (1.0 - saturation)
    zero_plane = jnp.zeros(saturation.shape[1:], jnp.float32)
    local_end, _ = lax.scan(descend, zero_plane, (retention, burden))
    through = jnp.prod(retention, axis=0)
    depth_size = lax.axis_size("gz")
    pair = jnp.stack([through, local_end])
    behind = [from_behind(pair, "gz", d) for d in range(1, depth_size)]
    entering = zero_plane
    for d in range(depth_size - 1, 0, -1):
        above = behind[d - 1]
        entering = above[0] * entering + above[1]
    _, inflow = lax.scan(descend, entering, (retention, burden))
    return inflow, burden


def on_device(saturation, retention, gravity, cell_map, owner_id, stream_dir, node_weight, flight):
    size_x = lax.axis_size("gx")
    size_y = lax.axis_size("gy")
    groups = size_x * size_y
    seg_len = cell_map.shape[2]
    capacity = cell_map.shape[1] // groups
    flat = saturation.reshape(-1)
    cell_count = flat.shape[0]
    map_rows = min(cell_count // 128, max(8, capacity * seg_len // 32))
    local_map = cell_map[0]

    offered = gather_cells(saturation, local_map, map_rows)
    arrived = lax.all_to_all(offered, ("gx", "gy"), split_axis=0, concat_axis=0, tiled=True)
    owners = owner_id[0, :, 0]
    rows = slot_rows(owners, groups, capacity)
    slots = groups * capacity
    filled = rows[None, :] == jnp.arange(slots, dtype=jnp.int32)[:, None]
    segments = rows.shape[0]
    weights = node_weight[0]
    halves = lax.broadcasted_iota(jnp.int32, (slots, 2, segments), 1)
    sat_rows = (filled[:, None, :] & (halves == 0)).reshape(2 * slots, segments)
    weight_rows = (filled[:, None, :] & (halves == 1)).reshape(2 * slots, segments)
    weight_part = jnp.dot(
        weight_rows.astype(jnp.float32),
        weights,
        precision=lax.Precision.HIGHEST,
        preferred_element_type=jnp.float32,
    )
    weight_part, arrived = lax.optimization_barrier((weight_part, arrived))
    node_in = jnp.dot(
        filled.T.astype(jnp.float32),
        arrived,
        precision=lax.Precision.HIGHEST,
        preferred_element_type=jnp.float32,
    )
    seg_dev = node_in.shape[0]
    updated = transport(
        node_in.reshape(seg_dev // 2, 2 * seg_len),
        flight[0].reshape(seg_dev // 2, 2 * seg_len),
        stream_dir[0],
    )
    updated = updated.reshape(seg_dev, seg_len)
    package = weight_part + jnp.dot(
        sat_rows.astype(jnp.float32),
        weights * updated,
        precision=lax.Precision.HIGHEST,
        preferred_element_type=jnp.float32,
    )
    returned = lax.all_to_all(package, ("gx", "gy"), split_axis=0, concat_axis=0, tiled=True)
    package, retention, gravity = lax.optimization_barrier((package, retention, gravity))
    inflow, burden = segregation(saturation, retention, gravity)
    final_sat = scatter_cells(local_map, returned, saturation, inflow, burden, map_rows)
    return (final_sat, updated[None])


def solution(mesh):
    return jax.shard_map(
        on_device,
        mesh=mesh,
        in_specs=(
            P("gz", "gx", "gy"),
            P("gz", "gx", "gy"),
            P("gz", "gx", "gy"),
            P("gz", ("gx", "gy"), None),
            P("gz", ("gx", "gy"), None),
            P("gz", ("gx", "gy")),
            P("gz", ("gx", "gy"), None),
            P("gz", ("gx", "gy"), None),
        ),
        out_specs=(P("gz", "gx", "gy"), P("gz", ("gx", "gy"), None)),
        check_vma=False,
    )
```

```python
import functools

import jax
import jax.numpy as jnp
from jax import lax
from jax.experimental import pallas as pl
from jax.experimental.pallas import tpu as pltpu
from jax.sharding import PartitionSpec as P


BL_STEPS = 8


def from_behind(block, axis, distance):
    devices = range(lax.axis_size(axis))
    route = [(i - distance, i) for i in devices if i - distance in devices]
    return lax.ppermute(block, axis, route)


def frac_flow(values):
    return values * values / (values * values + (1.0 - values) * (1.0 - values))


def transport(node_sat, increments, reversed_flag):
    flipped = reversed_flag[..., None] == 1
    state = node_sat
    inlet = jnp.ones(state.shape[:-1] + (1,), jnp.float32)
    for _ in range(BL_STEPS):
        flows = frac_flow(state)
        from_left = jnp.concatenate([inlet, flows[..., :-1]], axis=-1)
        from_right = jnp.concatenate([flows[..., 1:], inlet], axis=-1)
        upstream = jnp.where(flipped, from_right, from_left)
        state = state - increments * (flows - upstream)
    return state


def slot_rows(owners, groups, capacity):
    onehot = (owners[:, None] == jnp.arange(groups, dtype=jnp.int32)[None, :]).astype(jnp.int32)
    before = jnp.cumsum(onehot, axis=0) - onehot
    return owners * capacity + jnp.sum(before * onehot, axis=1)


def descend(carried, layer):
    keep, drop = layer
    inflow = keep * carried
    return (inflow + drop, inflow)


def gather_kernel(table_ref, ids_ref, out_ref):
    map_rows = table_ref.shape[1]
    tiles = ids_ref.shape[0] // 8
    table = table_ref[0]
    spread = [jnp.broadcast_to(table[r : r + 1, :], (8, 128)) for r in range(map_rows)]

    def body(i, carry):
        start = pl.multiple_of(i * 8, 8)
        ids = ids_ref[pl.ds(start, 8), :]
        lane = jnp.bitwise_and(ids, 127)
        level = jnp.right_shift(ids, 7)
        picked = jnp.zeros((8, 128), jnp.float32)
        for r in range(map_rows):
            got = jnp.take_along_axis(spread[r], lane, axis=1, mode="promise_in_bounds")
            picked = jnp.where(level == r, got, picked)
        out_ref[pl.ds(start, 8), :] = picked
        return carry

    lax.fori_loop(0, tiles, body, 0, unroll=True)


def gather_cells(saturation, local_map, map_rows):
    return pl.pallas_call(
        gather_kernel,
        out_shape=jax.ShapeDtypeStruct(local_map.shape, jnp.float32),
        grid=(2,),
        in_specs=[
            pl.BlockSpec((1, map_rows, 128), lambda i: (0, 0, 0)),
            pl.BlockSpec((local_map.shape[0] // 2, 128), lambda i: (i, 0)),
        ],
        out_specs=pl.BlockSpec((local_map.shape[0] // 2, 128), lambda i: (i, 0)),
    )(saturation, local_map)


def scatter_kernel(map_rows, ids_ref, both_ref, sat_ref, inflow_ref, burden_ref, out_ref):
    tiles = ids_ref.shape[0] // 8
    lanes = lax.broadcasted_iota(jnp.int32, (128, 128), 0)
    levels = lax.broadcasted_iota(jnp.int32, (map_rows, 128), 0)

    def pieces(values):
        high = values.astype(jnp.bfloat16)
        rest = values - high.astype(jnp.float32)
        middle = rest.astype(jnp.bfloat16)
        low = (rest - middle.astype(jnp.float32)).astype(jnp.bfloat16)
        return [high, middle, low]

    def body(i, totals):
        start = pl.multiple_of(i * 8, 8)
        ids = ids_ref[pl.ds(start, 8), :]
        upper = both_ref[pl.ds(2 * start, 8, stride=2), :]
        lower = both_ref[pl.ds(2 * start + 1, 8, stride=2), :]
        hots, parts = [], []
        for j in range(8):
            cell = ids[j : j + 1, :]
            hots.append((jnp.bitwise_and(cell, 127) == lanes).astype(jnp.bfloat16))
            on_level = jnp.right_shift(cell, 7) == levels
            rows = jnp.concatenate(
                [
                    jnp.where(on_level, upper[j : j + 1, :], 0.0),
                    jnp.where(on_level, lower[j : j + 1, :], 0.0),
                ],
                axis=0,
            )
            parts.append(jnp.concatenate(pieces(rows), axis=0))
        added = lax.dot_general(
            jnp.concatenate(parts, axis=1),
            jnp.concatenate(hots, axis=1),
            (((1,), (1,)), ((), ())),
            preferred_element_type=jnp.float32,
        )
        return totals + added

    totals = lax.fori_loop(
        0, tiles, body, jnp.zeros((6 * map_rows, 128), jnp.float32), unroll=True
    )
    span = 2 * map_rows
    summed = (totals[:span] + totals[span : 2 * span]) + totals[2 * span :]
    out_ref[...] = (sat_ref[...] + inflow_ref[...]) - burden_ref[...]
    mixed = (sat_ref[0, :map_rows, :] + summed[:map_rows]) / (1.0 + summed[map_rows:])
    out_ref[0, :map_rows, :] = (mixed + inflow_ref[0, :map_rows, :]) - burden_ref[0, :map_rows, :]


def scatter_cells(local_map, both, saturation, inflow, burden, map_rows):
    return pl.pallas_call(
        functools.partial(scatter_kernel, map_rows),
        out_shape=jax.ShapeDtypeStruct(saturation.shape, jnp.float32),
        in_specs=[pl.BlockSpec(memory_space=pltpu.VMEM)] * 5,
        out_specs=pl.BlockSpec(memory_space=pltpu.VMEM),
    )(local_map, both, saturation, inflow, burden)


def segregation(saturation, retention, gravity):
    burden = gravity * saturation * (1.0 - saturation)
    zero_plane = jnp.zeros(saturation.shape[1:], jnp.float32)
    local_end, _ = lax.scan(descend, zero_plane, (retention, burden))
    through = jnp.prod(retention, axis=0)
    depth_size = lax.axis_size("gz")
    pair = jnp.stack([through, local_end])
    behind = [from_behind(pair, "gz", d) for d in range(1, depth_size)]
    entering = zero_plane
    for d in range(depth_size - 1, 0, -1):
        above = behind[d - 1]
        entering = above[0] * entering + above[1]
    _, inflow = lax.scan(descend, entering, (retention, burden))
    return inflow, burden


def on_device(saturation, retention, gravity, cell_map, owner_id, stream_dir, node_weight, flight):
    size_x = lax.axis_size("gx")
    size_y = lax.axis_size("gy")
    groups = size_x * size_y
    seg_len = cell_map.shape[2]
    capacity = cell_map.shape[1] // groups
    flat = saturation.reshape(-1)
    cell_count = flat.shape[0]
    map_rows = min(cell_count // 128, max(8, capacity * seg_len // 32))
    local_map = cell_map[0]

    offered = gather_cells(saturation, local_map, map_rows)
    arrived = lax.all_to_all(offered, ("gx", "gy"), split_axis=0, concat_axis=0, tiled=True)
    owners = owner_id[0, :, 0]
    rows = slot_rows(owners, groups, capacity)
    slots = groups * capacity
    filled = rows[None, :] == jnp.arange(slots, dtype=jnp.int32)[:, None]
    segments = rows.shape[0]
    weights = node_weight[0]
    halves = lax.broadcasted_iota(jnp.int32, (slots, 2, segments), 1)
    sat_rows = (filled[:, None, :] & (halves == 0)).reshape(2 * slots, segments)
    weight_rows = (filled[:, None, :] & (halves == 1)).reshape(2 * slots, segments)
    weight_part = jnp.dot(
        weight_rows.astype(jnp.float32),
        weights,
        precision=lax.Precision.HIGHEST,
        preferred_element_type=jnp.float32,
    )
    weight_part, arrived = lax.optimization_barrier((weight_part, arrived))
    node_in = jnp.dot(
        filled.T.astype(jnp.float32),
        arrived,
        precision=lax.Precision.HIGHEST,
        preferred_element_type=jnp.float32,
    )
    seg_dev = node_in.shape[0]
    updated = transport(
        node_in.reshape(seg_dev // 2, 2 * seg_len),
        flight[0].reshape(seg_dev // 2, 2 * seg_len),
        stream_dir[0],
    )
    updated = updated.reshape(seg_dev, seg_len)
    package = weight_part + jnp.dot(
        sat_rows.astype(jnp.float32),
        weights * updated,
        precision=lax.Precision.HIGHEST,
        preferred_element_type=jnp.float32,
    )
    returned = lax.all_to_all(package, ("gx", "gy"), split_axis=0, concat_axis=0, tiled=True)
    package, retention, gravity = lax.optimization_barrier((package, retention, gravity))
    inflow, burden = segregation(saturation, retention, gravity)
    final_sat = scatter_cells(local_map, returned, saturation, inflow, burden, map_rows)
    return (final_sat, updated[None])


def solution(mesh):
    return jax.shard_map(
        on_device,
        mesh=mesh,
        in_specs=(
            P("gz", "gx", "gy"),
            P("gz", "gx", "gy"),
            P("gz", "gx", "gy"),
            P("gz", ("gx", "gy"), None),
            P("gz", ("gx", "gy"), None),
            P("gz", ("gx", "gy")),
            P("gz", ("gx", "gy"), None),
            P("gz", ("gx", "gy"), None),
        ),
        out_specs=(P("gz", "gx", "gy"), P("gz", ("gx", "gy"), None)),
        check_vma=False,
    )
```
